512 devices in a mesh: lon: 32 (over y_lo, z), lat: 16 (over x, y_hi, core).
Axes of the slice: x: 4, y: 4 (y_hi: 2, y_lo: 2; y = y_hi * 2 + y_lo), z: 16, core: 2. Of those that a mesh axis runs over, the one named last changes fastest.
Arguments:
- control: float32 [80, 512, 4096], P(None, 'lat', 'lon'), may hold values from -6 to 6
- diffusivity: float32 [512, 4096], P('lat', 'lon'), may hold values from 0.02 to 0.12
- land_mask: int32 [512, 4096], P('lat', 'lon'), may hold values 0 or 1
- innovations: float32 [16, 80, 4096], P('lat', None, 'lon'), may hold values from -6 to 6
- obs_sigma: float32 [16, 80, 4096], P('lat', None, 'lon'), may hold values from 0.5 to 2
- obs_row: int32 [16, 4096], P('lat', 'lon'), may hold values from 0 to 31
- obs_col: int32 [16, 4096], P('lat', 'lon'), may hold values from 0 to 127
- obs_frac: float32 [16, 2, 4096], P('lat', None, 'lon'), may hold values from 0 to 1
- obs_counts: int32 [16, 32], P('lat', 'lon'), may hold values from 32 to 128, as said below
Outputs:
- obs_gradient: float32 [80, 512, 4096], P(None, 'lat', 'lon')
- departures: float32 [16, 80, 4096], P('lat', None, 'lon')
The draws below stay inside these ranges and needn't reach their ends.
Inputs may be any that keep to these rules, and one draw needn't show every extreme that they name: `obs_counts`: every tile holds between 32 and 128 live profiles in its first slots; some tile holds exactly 128.
All inputs are finite; a program needn't handle non-finite values. No bound on the sum of `land_mask` on one device may be relied on, other than what follows from the above.
Results may differ from the reference program's by a relative error of at most 0.00002.
Values sent between devices are 32-bit elements; how exact they have to be, the bound alone decides.
No kernel may reach another device: no remote copies, remote signals or barrier semaphores. Data moves between devices by JAX's collectives and lax.ppermute only.
A program may use at most 64 MiB of HBM per device.

```python
import math
import jax
import jax.numpy as jnp
from jax import lax

TX = 128
TY = 32
VARS = 2
LEV = 40
OBS = 128
NX = 4096
NY = 512
N_LON = 32
N_LAT = 16


def draw_obs_counts(key, part):
    first_key, second_key = jax.random.split(jax.random.fold_in(key, 17))
    counts = jax.random.randint(first_key, (N_LAT, N_LON), OBS // 4, OBS + 1)
    chosen = jax.random.randint(second_key, (), 0, N_LAT * N_LON)
    places = jnp.arange(N_LAT * N_LON).reshape(N_LAT, N_LON)
    return jnp.where(places == chosen, OBS, counts).astype(jnp.int32)


def with_ends(values, stream_key, low, largest):
    index_at = [jax.random.randint(jax.random.fold_in(stream_key, axis), (), 0, length) for axis, length in enumerate(values.shape)]
    longest = values.shape.index(max(values.shape))
    beside = index_at[:longest] + [(index_at[longest] + 1) % values.shape[longest]] + index_at[longest + 1:]
    return values.at[tuple(index_at)].set(low).at[tuple(beside)].set(largest)


def level_of(stream_key, extent, cuts, least, top_value):
    def one(position, parts):
        steps = jax.random.uniform(jax.random.fold_in(jax.random.fold_in(stream_key, 6), position), (parts,), jnp.float32, least / len(cuts), top_value / len(cuts))
        return jnp.repeat(jnp.exp(steps), extent[position] // parts).reshape((-1,) + (1,) * (len(extent) - position - 1))

    factor_of = one(*cuts[0])
    for cut in cuts[1:]:
        factor_of = factor_of * one(*cut)
    return factor_of


def normal_values(stream_key, dims, scale, reach, shards=(), kind=jnp.bfloat16):
    drawn = scale * jax.random.normal(stream_key, dims, jnp.float32)
    if shards:
        drawn = drawn * level_of(stream_key, dims, shards, -0.22, 0.18)
    return jnp.clip(drawn, -reach, reach).astype(kind)


def setup_inputs(seed: int = 0) -> dict:
    splits = jax.random.split(jax.random.key(seed), 10)
    return {
        "control": normal_values(splits[0], (VARS * LEV, NY, NX), 1.0, 6.0, ((1, 16), (2, 32)), jnp.float32),
        "diffusivity": jnp.clip(jnp.exp(math.log(0.12) - 1.7917595 * jax.random.uniform(splits[1], (NY, NX), jnp.float32) ** level_of(splits[1], (NY, NX), ((0, 16), (1, 32)), -0.2, 0.2)), 0.02, 0.12),
        "land_mask": with_ends((jax.random.randint(splits[2], (NY, NX), 0, 10) < 7).astype(jnp.int32), jax.random.fold_in(splits[2], 1), 0, 1),
        "innovations": normal_values(splits[3], (N_LAT, VARS * LEV, N_LON * OBS), 1.0, 6.0, ((0, 16), (2, 32)), jnp.float32),
        "obs_sigma": jnp.clip(jnp.exp(math.log(2.0) - 1.3862944 * jax.random.uniform(splits[4], (N_LAT, VARS * LEV, N_LON * OBS), jnp.float32) ** level_of(splits[4], (N_LAT, VARS * LEV, N_LON * OBS), ((0, 16), (2, 32)), -0.2, 0.2)), 0.5, 2.0),
        "obs_row": with_ends(jax.random.randint(splits[5], (N_LAT, N_LON * OBS), 0, TY), jax.random.fold_in(splits[5], 1), 0, TY - 1).astype(jnp.int32),
        "obs_col": with_ends(jax.random.randint(splits[6], (N_LAT, N_LON * OBS), 0, TX), jax.random.fold_in(splits[6], 1), 0, TX - 1).astype(jnp.int32),
        "obs_frac": jnp.clip(1.0 * jax.random.uniform(splits[7], (N_LAT, 2, N_LON * OBS), jnp.float32) ** level_of(splits[7], (N_LAT, 2, N_LON * OBS), ((0, 16), (2, 32)), -0.2, 0.2), 0.0, 1.0),
        "obs_counts": draw_obs_counts(jax.random.fold_in(splits[9], 71), 0),
    }


def window(array, offset_y, offset_x):
    return array[..., 1 + offset_y: array.shape[-2] - 1 + offset_y, 1 + offset_x: array.shape[-1] - 1 + offset_x]


def diffuse(padded, kappa_pad, mask_pad):
    center = window(padded, 0, 0)
    kappa_mid = window(kappa_pad, 0, 0)
    mask_mid = window(mask_pad, 0, 0)
    result = center
    for offset_y, offset_x in ((0, 1), (0, -1), (1, 0), (-1, 0)):
        weight = 0.5 * (kappa_mid + window(kappa_pad, offset_y, offset_x)) * mask_mid * window(mask_pad, offset_y, offset_x)
        result = result + weight * (window(padded, offset_y, offset_x) - center)
    return result


def wrap_pad(field):
    joined = jnp.concatenate([field[:, -1:], field, field[:, :1]], axis=1)
    return jnp.pad(joined, ((1, 1), (0, 0)))


def reference(control, diffusivity, land_mask, innovations, obs_sigma, obs_row, obs_col, obs_frac, obs_counts):
    mask_float = land_mask.astype(jnp.float32)
    kappa_pad = wrap_pad(diffusivity)
    mask_pad = wrap_pad(mask_float)

    def smooth(field):
        for repeat in range(2):
            field = diffuse(wrap_pad(field), kappa_pad, mask_pad)
        return field

    lat_tile = jnp.broadcast_to(jnp.arange(N_LAT, dtype=jnp.int32)[:, None], obs_row.shape)
    column = jnp.broadcast_to(jnp.arange(N_LON * OBS, dtype=jnp.int32)[None, :], obs_row.shape)
    lon_tile = column // OBS
    slot_index = column % OBS
    grid_row = lat_tile * TY + obs_row + 1
    grid_col = lon_tile * TX + obs_col + 1
    valid = (slot_index < obs_counts[lat_tile, lon_tile]).astype(jnp.float32)
    frac_y = obs_frac[:, 0, :]
    frac_x = obs_frac[:, 1, :]
    stencil = ((0, 0, (1.0 - frac_y) * (1.0 - frac_x)), (0, 1, (1.0 - frac_y) * frac_x),
               (1, 0, frac_y * (1.0 - frac_x)), (1, 1, frac_y * frac_x))

    def level(inputs):
        field, innov, sigma = inputs
        state = smooth(field)
        padded = wrap_pad(state)
        sample = jnp.zeros_like(innov)
        for offset_y, offset_x, weight in stencil:
            sample = sample + weight * padded[grid_row + offset_y, grid_col + offset_x]
        departure = valid * (sample - innov)
        weighted = departure / (sigma * sigma)
        adjoint = jnp.zeros_like(padded)
        for offset_y, offset_x, weight in stencil:
            adjoint = adjoint.at[grid_row + offset_y, grid_col + offset_x].add(weight * weighted)
        inner = adjoint[1:-1, 1:-1]
        inner = inner.at[:, 0].add(adjoint[1:-1, -1])
        return smooth(inner), departure

    grads, departs = lax.map(level, (control, jnp.moveaxis(innovations, 1, 0), jnp.moveaxis(obs_sigma, 1, 0)))
    return grads, jnp.moveaxis(departs, 0, 1)
```

```python
import jax
import jax.numpy as jnp
from jax import lax
from jax.sharding import PartitionSpec as P

HN, HS, HW, HE = 3, 4, 3, 4
GN, GS, GW, GE = 2, 3, 2, 3


def neighbour_shift(block, dy, dx):
    n_lon = lax.axis_size("lon")
    n_lat = lax.axis_size("lat")
    if dy == 0:
        pairs = [((i + dx) % n_lon, i) for i in range(n_lon)]
        return lax.ppermute(block, "lon", pairs)
    if dx == 0:
        pairs = [(j + dy, j) for j in range(n_lat) if 0 <= j + dy < n_lat]
        return lax.ppermute(block, "lat", pairs)
    pairs = []
    for i in range(n_lon):
        for j in range(n_lat):
            if 0 <= j + dy < n_lat:
                source = ((i + dx) % n_lon) * n_lat + (j + dy)
                pairs.append((source, i * n_lat + j))
    return lax.ppermute(block, ("lon", "lat"), pairs)


def gather_halo(x, hn, hs, hw, he):
    rows, cols = x.shape[-2:]
    row_part = {-1: slice(rows - hn, rows), 0: slice(0, rows), 1: slice(0, hs)}
    col_part = {-1: slice(cols - hw, cols), 0: slice(0, cols), 1: slice(0, he)}
    grid = []
    for dy in (-1, 0, 1):
        line = []
        for dx in (-1, 0, 1):
            piece = x[..., row_part[dy], col_part[dx]]
            line.append(piece if dy == 0 and dx == 0 else neighbour_shift(piece, dy, dx))
        grid.append(jnp.concatenate(line, axis=-1))
    return jnp.concatenate(grid, axis=-2)


def scatter_halo(g, rows, cols, gn, gs, gw, ge):
    total = g[..., gn : gn + rows, gw : gw + cols]
    row_part = {-1: (slice(0, gn), slice(rows - gn, rows)),
                0: (slice(gn, gn + rows), slice(0, rows)),
                1: (slice(gn + rows, gn + rows + gs), slice(0, gs))}
    col_part = {-1: (slice(0, gw), slice(cols - gw, cols)),
                0: (slice(gw, gw + cols), slice(0, cols)),
                1: (slice(gw + cols, gw + cols + ge), slice(0, ge))}
    for dy in (-1, 0, 1):
        for dx in (-1, 0, 1):
            if dy == 0 and dx == 0:
                continue
            src_r, dst_r = row_part[dy]
            src_c, dst_c = col_part[dx]
            arrived = neighbour_shift(g[..., src_r, src_c], -dy, -dx)
            total = total.at[..., dst_r, dst_c].add(arrived)
    return total


def edge_weights(kappa, mask):
    mid = (slice(1, -1), slice(1, -1))
    kappa_mid = kappa[mid]
    mask_mid = mask[mid]
    out = []
    for oy, ox in ((0, 1), (0, -1), (1, 0), (-1, 0)):
        near = (slice(1 + oy, kappa.shape[0] - 1 + oy), slice(1 + ox, kappa.shape[1] - 1 + ox))
        out.append(0.5 * (kappa_mid + kappa[near]) * mask_mid * mask[near])
    return out


def diffuse(padded, weights):
    center = padded[..., 1:-1, 1:-1]
    result = center
    for (oy, ox), weight in zip(((0, 1), (0, -1), (1, 0), (-1, 0)), weights):
        near = padded[..., 1 + oy : padded.shape[-2] - 1 + oy, 1 + ox : padded.shape[-1] - 1 + ox]
        result = result + weight * (near - center)
    return result


def trim(weights, k):
    return [w[k : w.shape[0] - k, k : w.shape[1] - k] for w in weights]


def pad2(x, k):
    return jnp.pad(x, ((0, 0), (k, k), (k, k)))


def on_device(
    control, diffusivity, land_mask, innovations, obs_sigma, obs_row, obs_col, obs_frac, obs_counts
):
    channels, rows, cols = control.shape
    stacked = jnp.concatenate(
        [control, diffusivity[None], land_mask.astype(jnp.float32)[None]], axis=0
    )
    ext = gather_halo(stacked, HN, HS, HW, HE)
    field = ext[:channels]
    weights = edge_weights(ext[channels], ext[channels + 1])

    state = diffuse(diffuse(field, weights), trim(weights, 1))
    state = state[:, 1 : rows + 2, 1 : cols + 2]

    frac_y = obs_frac[0, 0]
    frac_x = obs_frac[0, 1]
    row_ids = lax.broadcasted_iota(jnp.int32, (rows + 1, obs_row.shape[1]), 0)
    col_ids = lax.broadcasted_iota(jnp.int32, (cols + 1, obs_col.shape[1]), 0)
    base_r = obs_row[0][None]
    base_c = obs_col[0][None]
    wy = jnp.where(row_ids == base_r, 1.0 - frac_y[None], 0.0) + jnp.where(
        row_ids == base_r + 1, frac_y[None], 0.0
    )
    wx = jnp.where(col_ids == base_c, 1.0 - frac_x[None], 0.0) + jnp.where(
        col_ids == base_c + 1, frac_x[None], 0.0
    )
    hi = lax.Precision.HIGHEST
    along = jnp.einsum("zrc,co->zro", state, wx, precision=hi)
    sample = jnp.sum(along * wy[None], axis=1)

    slots = jnp.arange(obs_row.shape[1], dtype=jnp.int32)
    valid = (slots < obs_counts[0, 0]).astype(jnp.float32)
    departure = valid * (sample - innovations[0])
    weighted = departure / (obs_sigma[0] * obs_sigma[0])

    spread = wy[None] * weighted[:, None, :]
    adjoint = jnp.einsum("zro,co->zrc", spread, wx, precision=hi)

    once = diffuse(pad2(adjoint, 2), trim(weights, 1))
    twice = diffuse(pad2(once, 2), weights)
    gradient = scatter_halo(twice, rows, cols, GN, GS, GW, GE)
    return gradient, departure[None]


def solution(mesh):
    in_specs = (
        P(None, "lat", "lon"),
        P("lat", "lon"),
        P("lat", "lon"),
        P("lat", None, "lon"),
        P("lat", None, "lon"),
        P("lat", "lon"),
        P("lat", "lon"),
        P("lat", None, "lon"),
        P("lat", "lon"),
    )
    out_specs = (P(None, "lat", "lon"), P("lat", None, "lon"))
    return jax.shard_map(
        on_device, mesh=mesh, in_specs=in_specs, out_specs=out_specs, check_vma=False
    )
```

```python
import jax
import jax.numpy as jnp
from jax import lax
from jax.sharding import PartitionSpec as P

HN, HS, HW, HE = 3, 4, 3, 4
GN, GS, GW, GE = 2, 3, 2, 3


def neighbour_shift(block, dy, dx):
    n_lon = lax.axis_size("lon")
    n_lat = lax.axis_size("lat")
    if dy == 0:
        pairs = [((i + dx) % n_lon, i) for i in range(n_lon)]
        return lax.ppermute(block, "lon", pairs)
    if dx == 0:
        pairs = [(j + dy, j) for j in range(n_lat) if 0 <= j + dy < n_lat]
        return lax.ppermute(block, "lat", pairs)
    pairs = []
    for i in range(n_lon):
        for j in range(n_lat):
            if 0 <= j + dy < n_lat:
                source = ((i + dx) % n_lon) * n_lat + (j + dy)
                pairs.append((source, i * n_lat + j))
    return lax.ppermute(block, ("lon", "lat"), pairs)


def gather_halo(x, hn, hs, hw, he):
    rows, cols = x.shape[-2:]
    west = neighbour_shift(x[..., :, cols - hw :], 0, -1)
    east = neighbour_shift(x[..., :, :he], 0, 1)
    x = jnp.concatenate([west, x, east], axis=-1)
    north = neighbour_shift(x[..., rows - hn :, :], -1, 0)
    south = neighbour_shift(x[..., :hs, :], 1, 0)
    return jnp.concatenate([north, x, south], axis=-2)


def scatter_halo(g, rows, cols, gn, gs, gw, ge):
    h = g[..., gn : gn + rows, :]
    from_south = neighbour_shift(g[..., :gn, :], 1, 0)
    from_north = neighbour_shift(g[..., gn + rows :, :], -1, 0)
    h = h.at[..., rows - gn :, :].add(from_south)
    h = h.at[..., :gs, :].add(from_north)
    total = h[..., :, gw : gw + cols]
    from_east = neighbour_shift(h[..., :, :gw], 0, 1)
    from_west = neighbour_shift(h[..., :, gw + cols :], 0, -1)
    total = total.at[..., :, cols - gw :].add(from_east)
    total = total.at[..., :, :ge].add(from_west)
    return total


def edge_weights(kappa, mask):
    mid = (slice(1, -1), slice(1, -1))
    kappa_mid = kappa[mid]
    mask_mid = mask[mid]
    out = []
    for oy, ox in ((0, 1), (0, -1), (1, 0), (-1, 0)):
        near = (slice(1 + oy, kappa.shape[0] - 1 + oy), slice(1 + ox, kappa.shape[1] - 1 + ox))
        out.append(0.5 * (kappa_mid + kappa[near]) * mask_mid * mask[near])
    return out


def diffuse(padded, weights):
    center = padded[..., 1:-1, 1:-1]
    result = center
    for (oy, ox), weight in zip(((0, 1), (0, -1), (1, 0), (-1, 0)), weights):
        near = padded[..., 1 + oy : padded.shape[-2] - 1 + oy, 1 + ox : padded.shape[-1] - 1 + ox]
        result = result + weight * (near - center)
    return result


def trim(weights, k):
    return [w[k : w.shape[0] - k, k : w.shape[1] - k] for w in weights]


def pad2(x, k):
    return jnp.pad(x, ((0, 0), (k, k), (k, k)))


def on_device(
    control, diffusivity, land_mask, innovations, obs_sigma, obs_row, obs_col, obs_frac, obs_counts
):
    channels, rows, cols = control.shape
    stacked = jnp.concatenate(
        [control, diffusivity[None], land_mask.astype(jnp.float32)[None]], axis=0
    )
    ext = gather_halo(stacked, HN, HS, HW, HE)
    field = ext[:channels]
    weights = edge_weights(ext[channels], ext[channels + 1])

    state = diffuse(diffuse(field, weights), trim(weights, 1))
    state = state[:, 1 : rows + 2, 1 : cols + 2]

    frac_y = obs_frac[0, 0]
    frac_x = obs_frac[0, 1]
    row_ids = lax.broadcasted_iota(jnp.int32, (rows + 1, obs_row.shape[1]), 0)
    col_ids = lax.broadcasted_iota(jnp.int32, (cols + 1, obs_col.shape[1]), 0)
    base_r = obs_row[0][None]
    base_c = obs_col[0][None]
    wy = jnp.where(row_ids == base_r, 1.0 - frac_y[None], 0.0) + jnp.where(
        row_ids == base_r + 1, frac_y[None], 0.0
    )
    wx = jnp.where(col_ids == base_c, 1.0 - frac_x[None], 0.0) + jnp.where(
        col_ids == base_c + 1, frac_x[None], 0.0
    )
    hi = lax.Precision.HIGHEST
    along = jnp.einsum("zrc,co->zro", state, wx, precision=hi)
    sample = jnp.sum(along * wy[None], axis=1)

    slots = jnp.arange(obs_row.shape[1], dtype=jnp.int32)
    valid = (slots < obs_counts[0, 0]).astype(jnp.float32)
    departure = valid * (sample - innovations[0])
    weighted = departure / (obs_sigma[0] * obs_sigma[0])

    spread = wy[None] * weighted[:, None, :]
    adjoint = jnp.einsum("zro,co->zrc", spread, wx, precision=hi)

    once = diffuse(pad2(adjoint, 2), trim(weights, 1))
    twice = diffuse(pad2(once, 2), weights)
    gradient = scatter_halo(twice, rows, cols, GN, GS, GW, GE)
    return gradient, departure[None]


def solution(mesh):
    in_specs = (
        P(None, "lat", "lon"),
        P("lat", "lon"),
        P("lat", "lon"),
        P("lat", None, "lon"),
        P("lat", None, "lon"),
        P("lat", "lon"),
        P("lat", "lon"),
        P("lat", None, "lon"),
        P("lat", "lon"),
    )
    out_specs = (P(None, "lat", "lon"), P("lat", None, "lon"))
    return jax.shard_map(
        on_device, mesh=mesh, in_specs=in_specs, out_specs=out_specs, check_vma=False
    )
```

```python
import jax
import jax.numpy as jnp
from jax import lax
from jax.sharding import PartitionSpec as P

HALO = 5


def neighbour_shift(block, dy, dx):
    n_lon = lax.axis_size("lon")
    n_lat = lax.axis_size("lat")
    if dy == 0:
        pairs = [((i + dx) % n_lon, i) for i in range(n_lon)]
        return lax.ppermute(block, "lon", pairs)
    if dx == 0:
        pairs = [(j + dy, j) for j in range(n_lat) if 0 <= j + dy < n_lat]
        return lax.ppermute(block, "lat", pairs)
    pairs = []
    for i in range(n_lon):
        for j in range(n_lat):
            if 0 <= j + dy < n_lat:
                source = ((i + dx) % n_lon) * n_lat + (j + dy)
                pairs.append((source, i * n_lat + j))
    return lax.ppermute(block, ("lon", "lat"), pairs)


def pack(arrays):
    return jnp.concatenate([a.reshape(-1) for a in arrays])


def unpack(flat, shapes):
    out, at = [], 0
    for shape in shapes:
        size = 1
        for n in shape:
            size *= n
        out.append(flat[at : at + size].reshape(shape))
        at += size
    return out


def exchange(x, obs, h):
    rows, cols = x.shape[-2:]
    side = x.shape[:-1] + (h,)
    east, obs_e = unpack(neighbour_shift(pack([x[..., :, :h], obs]), 0, 1), [side, obs.shape])
    west, obs_w = unpack(neighbour_shift(pack([x[..., :, cols - h :], obs]), 0, -1), [side, obs.shape])
    x = jnp.concatenate([west, x, east], axis=-1)
    line = jnp.stack([obs_w, obs, obs_e])
    band = x.shape[:-2] + (h, x.shape[-1])
    north, obs_n = unpack(
        neighbour_shift(pack([x[..., rows - h :, :], line]), -1, 0), [band, line.shape]
    )
    south, obs_s = unpack(neighbour_shift(pack([x[..., :h, :], line]), 1, 0), [band, line.shape])
    return jnp.concatenate([north, x, south], axis=-2), jnp.stack([obs_n, line, obs_s])


def edge_weights(kappa, mask):
    mid = (slice(1, -1), slice(1, -1))
    kappa_mid = kappa[mid]
    mask_mid = mask[mid]
    out = []
    for oy, ox in ((0, 1), (0, -1), (1, 0), (-1, 0)):
        near = (slice(1 + oy, kappa.shape[0] - 1 + oy), slice(1 + ox, kappa.shape[1] - 1 + ox))
        out.append(0.5 * (kappa_mid + kappa[near]) * mask_mid * mask[near])
    return out


def diffuse(padded, weights):
    center = padded[..., 1:-1, 1:-1]
    result = center
    for (oy, ox), weight in zip(((0, 1), (0, -1), (1, 0), (-1, 0)), weights):
        near = padded[..., 1 + oy : padded.shape[-2] - 1 + oy, 1 + ox : padded.shape[-1] - 1 + ox]
        result = result + weight * (near - center)
    return result


def trim(weights, k):
    return [w[k : w.shape[0] - k, k : w.shape[1] - k] for w in weights]


def on_device(
    control, diffusivity, land_mask, innovations, obs_sigma, obs_row, obs_col, obs_frac, obs_counts
):
    channels, rows, cols = control.shape
    n_obs = obs_row.shape[1]
    h = HALO
    stacked = jnp.concatenate(
        [control, diffusivity[None], land_mask.astype(jnp.float32)[None]], axis=0
    )
    slots = jnp.arange(n_obs, dtype=jnp.int32)
    valid = (slots < obs_counts[0, 0]).astype(jnp.float32)
    obs = jnp.concatenate(
        [
            innovations[0],
            obs_sigma[0] * obs_sigma[0],
            obs_row.astype(jnp.float32),
            obs_col.astype(jnp.float32),
            obs_frac[0],
            valid[None],
        ]
    )
    ext, every = exchange(stacked, obs, h)
    field = ext[:channels]
    weights = edge_weights(ext[channels], ext[channels + 1])

    state = diffuse(diffuse(field, weights), trim(weights, 1))
    lo = h - 2
    hi = lax.Precision.HIGHEST
    row_span = {-1: (-3, 1), 0: (0, rows + 1), 1: (rows, rows + 3)}
    col_span = {-1: (-3, 1), 0: (0, cols + 1), 1: (cols, cols + 3)}
    adjoint = jnp.zeros((channels, rows + 4, cols + 4), jnp.float32)
    departure = None
    for dy in (-1, 0, 1):
        for dx in (-1, 0, 1):
            data = every[1 + dy, 1 + dx]
            innov = data[:channels]
            s2 = data[channels : 2 * channels]
            base_r = data[2 * channels].astype(jnp.int32) + dy * rows
            base_c = data[2 * channels + 1].astype(jnp.int32) + dx * cols
            frac_y = data[2 * channels + 2]
            frac_x = data[2 * channels + 3]
            live = data[2 * channels + 4]
            r0, r1 = row_span[dy]
            c0, c1 = col_span[dx]
            row_ids = lax.broadcasted_iota(jnp.int32, (r1 - r0, n_obs), 0) + r0
            col_ids = lax.broadcasted_iota(jnp.int32, (c1 - c0, n_obs), 0) + c0
            wy = jnp.where(row_ids == base_r[None], 1.0 - frac_y[None], 0.0) + jnp.where(
                row_ids == base_r[None] + 1, frac_y[None], 0.0
            )
            wx = jnp.where(col_ids == base_c[None], 1.0 - frac_x[None], 0.0) + jnp.where(
                col_ids == base_c[None] + 1, frac_x[None], 0.0
            )
            region = state[:, lo + r0 : lo + r1, lo + c0 : lo + c1]
            along = jnp.einsum("zrc,co->zro", region, wx, precision=hi)
            sample = jnp.sum(along * wy[None], axis=1)
            depart = live[None] * (sample - innov)
            weighted = jnp.where(live[None] > 0, depart / jnp.where(s2 > 0, s2, 1.0), 0.0)
            part = jnp.einsum("zro,co->zrc", wy[None] * weighted[:, None, :], wx, precision=hi)
            a0, a1 = max(r0, -2), min(r1, rows + 2)
            b0, b1 = max(c0, -2), min(c1, cols + 2)
            part = part[:, a0 - r0 : a1 - r0, b0 - c0 : b1 - c0]
            adjoint = adjoint + jnp.pad(
                part, ((0, 0), (a0 + 2, rows + 2 - a1), (b0 + 2, cols + 2 - b1))
            )
            if dy == 0 and dx == 0:
                departure = depart

    once = diffuse(adjoint, trim(weights, h - 2))
    gradient = diffuse(once, trim(weights, h - 1))
    return gradient, departure[None]


def solution(mesh):
    in_specs = (
        P(None, "lat", "lon"),
        P("lat", "lon"),
        P("lat", "lon"),
        P("lat", None, "lon"),
        P("lat", None, "lon"),
        P("lat", "lon"),
        P("lat", "lon"),
        P("lat", None, "lon"),
        P("lat", "lon"),
    )
    out_specs = (P(None, "lat", "lon"), P("lat", None, "lon"))
    return jax.shard_map(
        on_device, mesh=mesh, in_specs=in_specs, out_specs=out_specs, check_vma=False
    )
```

```python
import jax
import jax.numpy as jnp
from jax import lax
from jax.sharding import PartitionSpec as P

HN, HS, HW, HE = 3, 4, 3, 4
GN, GS, GW, GE = 2, 3, 2, 3


def neighbour_shift(block, dy, dx):
    n_lon = lax.axis_size("lon")
    n_lat = lax.axis_size("lat")
    if dy == 0:
        pairs = [((i + dx) % n_lon, i) for i in range(n_lon)]
        return lax.ppermute(block, "lon", pairs)
    if dx == 0:
        pairs = [(j + dy, j) for j in range(n_lat) if 0 <= j + dy < n_lat]
        return lax.ppermute(block, "lat", pairs)
    pairs = []
    for i in range(n_lon):
        for j in range(n_lat):
            if 0 <= j + dy < n_lat:
                source = ((i + dx) % n_lon) * n_lat + (j + dy)
                pairs.append((source, i * n_lat + j))
    return lax.ppermute(block, ("lon", "lat"), pairs)


def gather_halo(x, split, hn, hs, hw, he):
    rows, cols = x.shape[-2:]
    west = neighbour_shift(x[..., :, cols - hw :], 0, -1)
    east = neighbour_shift(x[..., :, :he], 0, 1)
    edge_n = jnp.concatenate([west[..., rows - hn :, :], x[..., rows - hn :, :], east[..., rows - hn :, :]], axis=-1)
    edge_s = jnp.concatenate([west[..., :hs, :], x[..., :hs, :], east[..., :hs, :]], axis=-1)
    north = neighbour_shift(edge_n, -1, 0)
    south = neighbour_shift(edge_s, 1, 0)

    def assemble(part):
        middle = jnp.concatenate([west[part], x[part], east[part]], axis=-1)
        return jnp.concatenate([north[part], middle, south[part]], axis=-2)

    return assemble(slice(0, split)), assemble(slice(split, None))


def scatter_halo(g, rows, cols, gn, gs, gw, ge):
    h = g[..., gn : gn + rows, :]
    from_south = neighbour_shift(g[..., :gn, :], 1, 0)
    from_north = neighbour_shift(g[..., gn + rows :, :], -1, 0)
    h = h.at[..., rows - gn :, :].add(from_south)
    h = h.at[..., :gs, :].add(from_north)
    total = h[..., :, gw : gw + cols]
    from_east = neighbour_shift(h[..., :, :gw], 0, 1)
    from_west = neighbour_shift(h[..., :, gw + cols :], 0, -1)
    total = total.at[..., :, cols - gw :].add(from_east)
    total = total.at[..., :, :ge].add(from_west)
    return total


def edge_weights(kappa, mask):
    mid = (slice(1, -1), slice(1, -1))
    kappa_mid = kappa[mid]
    mask_mid = mask[mid]
    out = []
    for oy, ox in ((0, 1), (0, -1), (1, 0), (-1, 0)):
        near = (slice(1 + oy, kappa.shape[0] - 1 + oy), slice(1 + ox, kappa.shape[1] - 1 + ox))
        out.append(0.5 * (kappa_mid + kappa[near]) * mask_mid * mask[near])
    return out


def diffuse(padded, weights):
    center = padded[..., 1:-1, 1:-1]
    result = center
    for (oy, ox), weight in zip(((0, 1), (0, -1), (1, 0), (-1, 0)), weights):
        near = padded[..., 1 + oy : padded.shape[-2] - 1 + oy, 1 + ox : padded.shape[-1] - 1 + ox]
        result = result + weight * (near - center)
    return result


def trim(weights, k):
    return [w[k : w.shape[0] - k, k : w.shape[1] - k] for w in weights]


def pad2(x, k):
    return jnp.pad(x, ((0, 0), (k, k), (k, k)))


def on_device(
    control, diffusivity, land_mask, innovations, obs_sigma, obs_row, obs_col, obs_frac, obs_counts
):
    channels, rows, cols = control.shape
    stacked = jnp.concatenate(
        [control, diffusivity[None], land_mask.astype(jnp.float32)[None]], axis=0
    )
    field, coeff = gather_halo(stacked, channels, HN, HS, HW, HE)
    weights = edge_weights(coeff[0], coeff[1])

    state = diffuse(diffuse(field, weights), trim(weights, 1))
    state = state[:, 1 : rows + 2, 1 : cols + 2]
    state = lax.optimization_barrier(state)

    frac_y = obs_frac[0, 0]
    frac_x = obs_frac[0, 1]
    row_ids = lax.broadcasted_iota(jnp.int32, (rows + 1, obs_row.shape[1]), 0)
    col_ids = lax.broadcasted_iota(jnp.int32, (cols + 1, obs_col.shape[1]), 0)
    base_r = obs_row[0][None]
    base_c = obs_col[0][None]
    wy = jnp.where(row_ids == base_r, 1.0 - frac_y[None], 0.0) + jnp.where(
        row_ids == base_r + 1, frac_y[None], 0.0
    )
    wx = jnp.where(col_ids == base_c, 1.0 - frac_x[None], 0.0) + jnp.where(
        col_ids == base_c + 1, frac_x[None], 0.0
    )
    hi = lax.Precision.HIGHEST
    along = jnp.einsum("zrc,co->zro", state, wx, precision=hi)
    sample = jnp.sum(along * wy[None], axis=1)

    slots = jnp.arange(obs_row.shape[1], dtype=jnp.int32)
    valid = (slots < obs_counts[0, 0]).astype(jnp.float32)
    departure = valid * (sample - innovations[0])
    weighted = departure / (obs_sigma[0] * obs_sigma[0])

    spread = wy[None] * weighted[:, None, :]
    adjoint = jnp.einsum("zro,co->zrc", spread, wx, precision=hi)
    adjoint = lax.optimization_barrier(adjoint)

    once = diffuse(pad2(adjoint, 2), trim(weights, 1))
    twice = diffuse(pad2(once, 2), weights)
    gradient = scatter_halo(twice, rows, cols, GN, GS, GW, GE)
    return gradient, departure[None]


def solution(mesh):
    in_specs = (
        P(None, "lat", "lon"),
        P("lat", "lon"),
        P("lat", "lon"),
        P("lat", None, "lon"),
        P("lat", None, "lon"),
        P("lat", "lon"),
        P("lat", "lon"),
        P("lat", None, "lon"),
        P("lat", "lon"),
    )
    out_specs = (P(None, "lat", "lon"), P("lat", None, "lon"))
    return jax.shard_map(
        on_device, mesh=mesh, in_specs=in_specs, out_specs=out_specs, check_vma=False
    )
```

```python
import jax
import jax.numpy as jnp
from jax import lax
from jax.sharding import PartitionSpec as P

HN, HS, HW, HE = 3, 4, 3, 4
GN, GS, GW, GE = 2, 3, 2, 3


def neighbour_shift(block, dy, dx):
    n_lon = lax.axis_size("lon")
    n_lat = lax.axis_size("lat")
    if dy == 0:
        pairs = [((i + dx) % n_lon, i) for i in range(n_lon)]
        return lax.ppermute(block, "lon", pairs)
    if dx == 0:
        pairs = [(j + dy, j) for j in range(n_lat) if 0 <= j + dy < n_lat]
        return lax.ppermute(block, "lat", pairs)
    pairs = []
    for i in range(n_lon):
        for j in range(n_lat):
            if 0 <= j + dy < n_lat:
                source = ((i + dx) % n_lon) * n_lat + (j + dy)
                pairs.append((source, i * n_lat + j))
    return lax.ppermute(block, ("lon", "lat"), pairs)


def gather_halo(parts, hn, hs, hw, he):
    rows, cols = parts[0].shape[-2:]
    sizes = [p.shape[0] for p in parts]

    def joined(window):
        return jnp.concatenate([p[window] for p in parts], axis=0)

    west = neighbour_shift(joined((Ellipsis, slice(None), slice(cols - hw, None))), 0, -1)
    east = neighbour_shift(joined((Ellipsis, slice(None), slice(0, he))), 0, 1)
    edge_n = jnp.concatenate(
        [west[..., rows - hn :, :], joined((Ellipsis, slice(rows - hn, None), slice(None))),
         east[..., rows - hn :, :]], axis=-1)
    edge_s = jnp.concatenate(
        [west[..., :hs, :], joined((Ellipsis, slice(0, hs), slice(None))), east[..., :hs, :]], axis=-1)
    north = neighbour_shift(edge_n, -1, 0)
    south = neighbour_shift(edge_s, 1, 0)

    out, at = [], 0
    for part, size in zip(parts, sizes):
        span = slice(at, at + size)
        middle = jnp.concatenate([west[span], part, east[span]], axis=-1)
        out.append(jnp.concatenate([north[span], middle, south[span]], axis=-2))
        at += size
    return out


def scatter_halo(g, rows, cols, gn, gs, gw, ge):
    h = g[..., gn : gn + rows, :]
    from_south = neighbour_shift(g[..., :gn, :], 1, 0)
    from_north = neighbour_shift(g[..., gn + rows :, :], -1, 0)
    h = h.at[..., rows - gn :, :].add(from_south)
    h = h.at[..., :gs, :].add(from_north)
    total = h[..., :, gw : gw + cols]
    from_east = neighbour_shift(h[..., :, :gw], 0, 1)
    from_west = neighbour_shift(h[..., :, gw + cols :], 0, -1)
    total = total.at[..., :, cols - gw :].add(from_east)
    total = total.at[..., :, :ge].add(from_west)
    return total


def edge_weights(kappa, mask):
    mid = (slice(1, -1), slice(1, -1))
    kappa_mid = kappa[mid]
    mask_mid = mask[mid]
    out = []
    for oy, ox in ((0, 1), (0, -1), (1, 0), (-1, 0)):
        near = (slice(1 + oy, kappa.shape[0] - 1 + oy), slice(1 + ox, kappa.shape[1] - 1 + ox))
        out.append(0.5 * (kappa_mid + kappa[near]) * mask_mid * mask[near])
    return out


def diffuse(padded, weights):
    center = padded[..., 1:-1, 1:-1]
    result = center
    for (oy, ox), weight in zip(((0, 1), (0, -1), (1, 0), (-1, 0)), weights):
        near = padded[..., 1 + oy : padded.shape[-2] - 1 + oy, 1 + ox : padded.shape[-1] - 1 + ox]
        result = result + weight * (near - center)
    return result


def trim(weights, k):
    return [w[k : w.shape[0] - k, k : w.shape[1] - k] for w in weights]


def pad2(x, k):
    return jnp.pad(x, ((0, 0), (k, k), (k, k)))


def on_device(
    control, diffusivity, land_mask, innovations, obs_sigma, obs_row, obs_col, obs_frac, obs_counts
):
    channels, rows, cols = control.shape
    coeff = jnp.stack([diffusivity, land_mask.astype(jnp.float32)])
    field, coeff = gather_halo([control, coeff], HN, HS, HW, HE)
    weights = edge_weights(coeff[0], coeff[1])

    state = diffuse(diffuse(field, weights), trim(weights, 1))
    state = state[:, 1 : rows + 2, 1 : cols + 2]
    state = lax.optimization_barrier(state)

    frac_y = obs_frac[0, 0]
    frac_x = obs_frac[0, 1]
    row_ids = lax.broadcasted_iota(jnp.int32, (rows + 1, obs_row.shape[1]), 0)
    col_ids = lax.broadcasted_iota(jnp.int32, (cols + 1, obs_col.shape[1]), 0)
    base_r = obs_row[0][None]
    base_c = obs_col[0][None]
    wy = jnp.where(row_ids == base_r, 1.0 - frac_y[None], 0.0) + jnp.where(
        row_ids == base_r + 1, frac_y[None], 0.0
    )
    wx = jnp.where(col_ids == base_c, 1.0 - frac_x[None], 0.0) + jnp.where(
        col_ids == base_c + 1, frac_x[None], 0.0
    )
    hi = lax.Precision.HIGHEST
    along = jnp.einsum("zrc,co->zro", state, wx, precision=hi)
    sample = jnp.sum(along * wy[None], axis=1)

    slots = jnp.arange(obs_row.shape[1], dtype=jnp.int32)
    valid = (slots < obs_counts[0, 0]).astype(jnp.float32)
    departure = valid * (sample - innovations[0])
    weighted = departure / (obs_sigma[0] * obs_sigma[0])

    spread = wy[None] * weighted[:, None, :]
    adjoint = jnp.einsum("zro,co->zrc", spread, wx, precision=hi)
    adjoint = lax.optimization_barrier(adjoint)

    once = diffuse(pad2(adjoint, 2), trim(weights, 1))
    twice = diffuse(pad2(once, 2), weights)
    gradient = scatter_halo(twice, rows, cols, GN, GS, GW, GE)
    return gradient, departure[None]


def solution(mesh):
    in_specs = (
        P(None, "lat", "lon"),
        P("lat", "lon"),
        P("lat", "lon"),
        P("lat", None, "lon"),
        P("lat", None, "lon"),
        P("lat", "lon"),
        P("lat", "lon"),
        P("lat", None, "lon"),
        P("lat", "lon"),
    )
    out_specs = (P(None, "lat", "lon"), P("lat", None, "lon"))
    return jax.shard_map(
        on_device, mesh=mesh, in_specs=in_specs, out_specs=out_specs, check_vma=False
    )
```

```python
import jax
import jax.numpy as jnp
from jax import lax
from jax.sharding import PartitionSpec as P

HN, HS, HW, HE = 3, 4, 3, 4
GN, GS, GW, GE = 2, 3, 2, 3


def neighbour_shift(block, dy, dx):
    n_lon = lax.axis_size("lon")
    n_lat = lax.axis_size("lat")
    if dy == 0:
        pairs = [((i + dx) % n_lon, i) for i in range(n_lon)]
        return lax.ppermute(block, "lon", pairs)
    if dx == 0:
        pairs = [(j + dy, j) for j in range(n_lat) if 0 <= j + dy < n_lat]
        return lax.ppermute(block, "lat", pairs)
    pairs = []
    for i in range(n_lon):
        for j in range(n_lat):
            if 0 <= j + dy < n_lat:
                source = ((i + dx) % n_lon) * n_lat + (j + dy)
                pairs.append((source, i * n_lat + j))
    return lax.ppermute(block, ("lon", "lat"), pairs)


def gather_halo(parts, hn, hs, hw, he):
    rows, cols = parts[0].shape[-2:]
    sizes = [p.shape[0] for p in parts]

    def joined(window):
        return jnp.concatenate([p[window] for p in parts], axis=0)

    west = neighbour_shift(joined((Ellipsis, slice(None), slice(cols - hw, None))), 0, -1)
    east = neighbour_shift(joined((Ellipsis, slice(None), slice(0, he))), 0, 1)
    edge_n = jnp.concatenate(
        [west[..., rows - hn :, :], joined((Ellipsis, slice(rows - hn, None), slice(None))),
         east[..., rows - hn :, :]], axis=-1)
    edge_s = jnp.concatenate(
        [west[..., :hs, :], joined((Ellipsis, slice(0, hs), slice(None))), east[..., :hs, :]], axis=-1)
    north = neighbour_shift(edge_n, -1, 0)
    south = neighbour_shift(edge_s, 1, 0)

    out, at = [], 0
    for part, size in zip(parts, sizes):
        span = slice(at, at + size)
        middle = jnp.concatenate([west[span], part, east[span]], axis=-1)
        out.append(jnp.concatenate([north[span], middle, south[span]], axis=-2))
        at += size
    return out


def scatter_halo(g, rows, cols, gn, gs, gw, ge):
    h = g[..., gn : gn + rows, :]
    from_south = neighbour_shift(g[..., :gn, :], 1, 0)
    from_north = neighbour_shift(g[..., gn + rows :, :], -1, 0)
    h = h.at[..., rows - gn :, :].add(from_south)
    h = h.at[..., :gs, :].add(from_north)
    total = h[..., :, gw : gw + cols]
    from_east = neighbour_shift(h[..., :, :gw], 0, 1)
    from_west = neighbour_shift(h[..., :, gw + cols :], 0, -1)
    total = total.at[..., :, cols - gw :].add(from_east)
    total = total.at[..., :, :ge].add(from_west)
    return total


def edge_weights(kappa, mask):
    mid = (slice(1, -1), slice(1, -1))
    kappa_mid = kappa[mid]
    mask_mid = mask[mid]
    out = []
    for oy, ox in ((0, 1), (0, -1), (1, 0), (-1, 0)):
        near = (slice(1 + oy, kappa.shape[0] - 1 + oy), slice(1 + ox, kappa.shape[1] - 1 + ox))
        out.append(0.5 * (kappa_mid + kappa[near]) * mask_mid * mask[near])
    return out


def diffuse(padded, weights):
    center = padded[..., 1:-1, 1:-1]
    result = center
    for (oy, ox), weight in zip(((0, 1), (0, -1), (1, 0), (-1, 0)), weights):
        near = padded[..., 1 + oy : padded.shape[-2] - 1 + oy, 1 + ox : padded.shape[-1] - 1 + ox]
        result = result + weight * (near - center)
    return result


def trim(weights, k):
    return [w[k : w.shape[0] - k, k : w.shape[1] - k] for w in weights]


def pad2(x, k):
    return jnp.pad(x, ((0, 0), (k, k), (k, k)))


def on_device(
    control, diffusivity, land_mask, innovations, obs_sigma, obs_row, obs_col, obs_frac, obs_counts
):
    channels, rows, cols = control.shape
    coeff = jnp.stack([diffusivity, land_mask.astype(jnp.float32)])
    field, coeff = gather_halo([control, coeff], HN, HS, HW, HE)
    weights = edge_weights(coeff[0], coeff[1])

    once = diffuse(field, weights)
    state = diffuse(
        once[:, 1 : rows + 4, 1 : cols + 4], [w[2 : rows + 3, 2 : cols + 3] for w in weights]
    )
    state = lax.optimization_barrier(state)

    frac_y = obs_frac[0, 0]
    frac_x = obs_frac[0, 1]
    row_ids = lax.broadcasted_iota(jnp.int32, (rows + 1, obs_row.shape[1]), 0)
    col_ids = lax.broadcasted_iota(jnp.int32, (cols + 1, obs_col.shape[1]), 0)
    base_r = obs_row[0][None]
    base_c = obs_col[0][None]
    wy = jnp.where(row_ids == base_r, 1.0 - frac_y[None], 0.0) + jnp.where(
        row_ids == base_r + 1, frac_y[None], 0.0
    )
    wx = jnp.where(col_ids == base_c, 1.0 - frac_x[None], 0.0) + jnp.where(
        col_ids == base_c + 1, frac_x[None], 0.0
    )
    hi = lax.Precision.HIGHEST
    along = jnp.einsum("zrc,co->zro", state, wx, precision=hi)
    sample = jnp.sum(along * wy[None], axis=1)

    slots = jnp.arange(obs_row.shape[1], dtype=jnp.int32)
    valid = (slots < obs_counts[0, 0]).astype(jnp.float32)
    departure = valid * (sample - innovations[0])
    weighted = departure / (obs_sigma[0] * obs_sigma[0])

    spread = wy[None] * weighted[:, None, :]
    adjoint = jnp.einsum("zro,co->zrc", spread, wx, precision=hi)
    adjoint = lax.optimization_barrier(adjoint)

    once = diffuse(pad2(adjoint, 2), trim(weights, 1))
    twice = diffuse(pad2(once, 2), weights)
    gradient = scatter_halo(twice, rows, cols, GN, GS, GW, GE)
    return gradient, departure[None]


def solution(mesh):
    in_specs = (
        P(None, "lat", "lon"),
        P("lat", "lon"),
        P("lat", "lon"),
        P("lat", None, "lon"),
        P("lat", None, "lon"),
        P("lat", "lon"),
        P("lat", "lon"),
        P("lat", None, "lon"),
        P("lat", "lon"),
    )
    out_specs = (P(None, "lat", "lon"), P("lat", None, "lon"))
    return jax.shard_map(
        on_device, mesh=mesh, in_specs=in_specs, out_specs=out_specs, check_vma=False
    )
```

```python
import jax
import jax.numpy as jnp
from jax import lax
from jax.sharding import PartitionSpec as P

HN, HS, HW, HE = 3, 4, 3, 4
GN, GS, GW, GE = 2, 3, 2, 3


def neighbour_shift(block, dy, dx):
    n_lon = lax.axis_size("lon")
    n_lat = lax.axis_size("lat")
    if dy == 0:
        pairs = [((i + dx) % n_lon, i) for i in range(n_lon)]
        return lax.ppermute(block, "lon", pairs)
    if dx == 0:
        pairs = [(j + dy, j) for j in range(n_lat) if 0 <= j + dy < n_lat]
        return lax.ppermute(block, "lat", pairs)
    pairs = []
    for i in range(n_lon):
        for j in range(n_lat):
            if 0 <= j + dy < n_lat:
                source = ((i + dx) % n_lon) * n_lat + (j + dy)
                pairs.append((source, i * n_lat + j))
    return lax.ppermute(block, ("lon", "lat"), pairs)


def gather_halo(parts, hn, hs, hw, he):
    rows, cols = parts[0].shape[-2:]
    sizes = [p.shape[0] for p in parts]

    def joined(window):
        return jnp.concatenate([p[window] for p in parts], axis=0)

    west = neighbour_shift(joined((Ellipsis, slice(None), slice(cols - hw, None))), 0, -1)
    east = neighbour_shift(joined((Ellipsis, slice(None), slice(0, he))), 0, 1)
    edge_n = jnp.concatenate(
        [west[..., rows - hn :, :], joined((Ellipsis, slice(rows - hn, None), slice(None))),
         east[..., rows - hn :, :]], axis=-1)
    edge_s = jnp.concatenate(
        [west[..., :hs, :], joined((Ellipsis, slice(0, hs), slice(None))), east[..., :hs, :]], axis=-1)
    north = neighbour_shift(edge_n, -1, 0)
    south = neighbour_shift(edge_s, 1, 0)

    out, at = [], 0
    for part, size in zip(parts, sizes):
        span = slice(at, at + size)
        middle = jnp.concatenate([west[span], part, east[span]], axis=-1)
        out.append(jnp.concatenate([north[span], middle, south[span]], axis=-2))
        at += size
    return out


def scatter_halo(g, rows, cols, gn, gs, gw, ge):
    h = g[..., gn : gn + rows, :]
    from_south = neighbour_shift(g[..., :gn, :], 1, 0)
    from_north = neighbour_shift(g[..., gn + rows :, :], -1, 0)
    h = h.at[..., rows - gn :, :].add(from_south)
    h = h.at[..., :gs, :].add(from_north)
    total = h[..., :, gw : gw + cols]
    from_east = neighbour_shift(h[..., :, :gw], 0, 1)
    from_west = neighbour_shift(h[..., :, gw + cols :], 0, -1)
    total = total.at[..., :, cols - gw :].add(from_east)
    total = total.at[..., :, :ge].add(from_west)
    return total


def edge_weights(kappa, mask):
    mid = (slice(1, -1), slice(1, -1))
    kappa_mid = kappa[mid]
    mask_mid = mask[mid]
    out = []
    for oy, ox in ((0, 1), (0, -1), (1, 0), (-1, 0)):
        near = (slice(1 + oy, kappa.shape[0] - 1 + oy), slice(1 + ox, kappa.shape[1] - 1 + ox))
        out.append(0.5 * (kappa_mid + kappa[near]) * mask_mid * mask[near])
    return [1.0 - (((out[0] + out[1]) + out[2]) + out[3])] + out


def diffuse(padded, weights):
    result = weights[0] * padded[..., 1:-1, 1:-1]
    for (oy, ox), weight in zip(((0, 1), (0, -1), (1, 0), (-1, 0)), weights[1:]):
        near = padded[..., 1 + oy : padded.shape[-2] - 1 + oy, 1 + ox : padded.shape[-1] - 1 + ox]
        result = result + weight * near
    return result


def trim(weights, k):
    return [w[k : w.shape[0] - k, k : w.shape[1] - k] for w in weights]


def pad2(x, k):
    return jnp.pad(x, ((0, 0), (k, k), (k, k)))


def on_device(
    control, diffusivity, land_mask, innovations, obs_sigma, obs_row, obs_col, obs_frac, obs_counts
):
    channels, rows, cols = control.shape
    coeff = jnp.stack([diffusivity, land_mask.astype(jnp.float32)])
    field, coeff = gather_halo([control, coeff], HN, HS, HW, HE)
    weights = edge_weights(coeff[0], coeff[1])

    once = diffuse(field, weights)
    state = diffuse(
        once[:, 1 : rows + 4, 1 : cols + 4], [w[2 : rows + 3, 2 : cols + 3] for w in weights]
    )
    state = lax.optimization_barrier(state)

    frac_y = obs_frac[0, 0]
    frac_x = obs_frac[0, 1]
    row_ids = lax.broadcasted_iota(jnp.int32, (rows + 1, obs_row.shape[1]), 0)
    col_ids = lax.broadcasted_iota(jnp.int32, (cols + 1, obs_col.shape[1]), 0)
    base_r = obs_row[0][None]
    base_c = obs_col[0][None]
    wy = jnp.where(row_ids == base_r, 1.0 - frac_y[None], 0.0) + jnp.where(
        row_ids == base_r + 1, frac_y[None], 0.0
    )
    wx = jnp.where(col_ids == base_c, 1.0 - frac_x[None], 0.0) + jnp.where(
        col_ids == base_c + 1, frac_x[None], 0.0
    )
    hi = lax.Precision.HIGHEST
    along = jnp.einsum("zrc,co->zro", state, wx, precision=hi)
    sample = jnp.sum(along * wy[None], axis=1)

    slots = jnp.arange(obs_row.shape[1], dtype=jnp.int32)
    valid = (slots < obs_counts[0, 0]).astype(jnp.float32)
    departure = valid * (sample - innovations[0])
    weighted = departure / (obs_sigma[0] * obs_sigma[0])

    spread = wy[None] * weighted[:, None, :]
    adjoint = jnp.einsum("zro,co->zrc", spread, wx, precision=hi)
    adjoint = lax.optimization_barrier(adjoint)

    once = diffuse(pad2(adjoint, 2), trim(weights, 1))
    twice = diffuse(pad2(once, 2), weights)
    gradient = scatter_halo(twice, rows, cols, GN, GS, GW, GE)
    return gradient, departure[None]


def solution(mesh):
    in_specs = (
        P(None, "lat", "lon"),
        P("lat", "lon"),
        P("lat", "lon"),
        P("lat", None, "lon"),
        P("lat", None, "lon"),
        P("lat", "lon"),
        P("lat", "lon"),
        P("lat", None, "lon"),
        P("lat", "lon"),
    )
    out_specs = (P(None, "lat", "lon"), P("lat", None, "lon"))
    return jax.shard_map(
        on_device, mesh=mesh, in_specs=in_specs, out_specs=out_specs, check_vma=False
    )
```

```python
import jax
import jax.numpy as jnp
from jax import lax
from jax.sharding import PartitionSpec as P

HN, HS, HW, HE = 3, 4, 3, 4
GN, GS, GW, GE = 2, 3, 2, 3


def neighbour_shift(block, dy, dx):
    n_lon = lax.axis_size("lon")
    n_lat = lax.axis_size("lat")
    if dy == 0:
        pairs = [((i + dx) % n_lon, i) for i in range(n_lon)]
        return lax.ppermute(block, "lon", pairs)
    if dx == 0:
        pairs = [(j + dy, j) for j in range(n_lat) if 0 <= j + dy < n_lat]
        return lax.ppermute(block, "lat", pairs)
    pairs = []
    for i in range(n_lon):
        for j in range(n_lat):
            if 0 <= j + dy < n_lat:
                source = ((i + dx) % n_lon) * n_lat + (j + dy)
                pairs.append((source, i * n_lat + j))
    return lax.ppermute(block, ("lon", "lat"), pairs)


def gather_halo(parts, hn, hs, hw, he):
    rows, cols = parts[0].shape[-2:]
    sizes = [p.shape[0] for p in parts]

    def joined(window):
        return jnp.concatenate([p[window] for p in parts], axis=0)

    west = neighbour_shift(joined((Ellipsis, slice(None), slice(cols - hw, None))), 0, -1)
    east = neighbour_shift(joined((Ellipsis, slice(None), slice(0, he))), 0, 1)
    edge_n = jnp.concatenate(
        [west[..., rows - hn :, :], joined((Ellipsis, slice(rows - hn, None), slice(None))),
         east[..., rows - hn :, :]], axis=-1)
    edge_s = jnp.concatenate(
        [west[..., :hs, :], joined((Ellipsis, slice(0, hs), slice(None))), east[..., :hs, :]], axis=-1)
    north = neighbour_shift(edge_n, -1, 0)
    south = neighbour_shift(edge_s, 1, 0)

    out, at = [], 0
    for part, size in zip(parts, sizes):
        span = slice(at, at + size)
        middle = jnp.concatenate([west[span], part, east[span]], axis=-1)
        out.append(jnp.concatenate([north[span], middle, south[span]], axis=-2))
        at += size
    return out


def scatter_halo(g, rows, cols, gn, gs, gw, ge):
    h = g[..., gn : gn + rows, :]
    from_south = neighbour_shift(g[..., :gn, :], 1, 0)
    from_north = neighbour_shift(g[..., gn + rows :, :], -1, 0)
    h = h.at[..., rows - gn :, :].add(from_south)
    h = h.at[..., :gs, :].add(from_north)
    total = h[..., :, gw : gw + cols]
    from_east = neighbour_shift(h[..., :, :gw], 0, 1)
    from_west = neighbour_shift(h[..., :, gw + cols :], 0, -1)
    total = total.at[..., :, cols - gw :].add(from_east)
    total = total.at[..., :, :ge].add(from_west)
    return total


def edge_weights(kappa, mask):
    mid = (slice(1, -1), slice(1, -1))
    kappa_mid = kappa[mid]
    mask_mid = mask[mid]
    out = []
    for oy, ox in ((0, 1), (0, -1), (1, 0), (-1, 0)):
        near = (slice(1 + oy, kappa.shape[0] - 1 + oy), slice(1 + ox, kappa.shape[1] - 1 + ox))
        out.append(0.5 * (kappa_mid + kappa[near]) * mask_mid * mask[near])
    return out


def diffuse(padded, weights):
    center = padded[..., 1:-1, 1:-1]
    result = center
    for (oy, ox), weight in zip(((0, 1), (0, -1), (1, 0), (-1, 0)), weights):
        near = padded[..., 1 + oy : padded.shape[-2] - 1 + oy, 1 + ox : padded.shape[-1] - 1 + ox]
        result = result + weight * (near - center)
    return result


def trim(weights, k):
    return [w[k : w.shape[0] - k, k : w.shape[1] - k] for w in weights]


def pad2(x, k):
    return jnp.pad(x, ((0, 0), (k, k), (k, k)))


def on_device(
    control, diffusivity, land_mask, innovations, obs_sigma, obs_row, obs_col, obs_frac, obs_counts
):
    channels, rows, cols = control.shape
    coeff = jnp.stack([diffusivity, land_mask.astype(jnp.float32)])
    field, coeff = gather_halo([control, coeff], HN, HS, HW, HE)
    weights = edge_weights(coeff[0], coeff[1])

    once = diffuse(field, weights)
    state = diffuse(
        once[:, 1 : rows + 4, 1 : cols + 4], [w[2 : rows + 3, 2 : cols + 3] for w in weights]
    )
    state = lax.optimization_barrier(state)

    frac_y = obs_frac[0, 0]
    frac_x = obs_frac[0, 1]
    row_ids = lax.broadcasted_iota(jnp.int32, (rows + 1, obs_row.shape[1]), 0)
    col_ids = lax.broadcasted_iota(jnp.int32, (cols + 1, obs_col.shape[1]), 0)
    base_r = obs_row[0][None]
    base_c = obs_col[0][None]
    wy = jnp.where(row_ids == base_r, 1.0 - frac_y[None], 0.0) + jnp.where(
        row_ids == base_r + 1, frac_y[None], 0.0
    )
    wx = jnp.where(col_ids == base_c, 1.0 - frac_x[None], 0.0) + jnp.where(
        col_ids == base_c + 1, frac_x[None], 0.0
    )
    hi = lax.Precision.HIGHEST
    along = jnp.einsum("zrc,co->zro", state, wx, precision=hi)
    sample = jnp.sum(along * wy[None], axis=1)

    slots = jnp.arange(obs_row.shape[1], dtype=jnp.int32)
    valid = (slots < obs_counts[0, 0]).astype(jnp.float32)
    departure = valid * (sample - innovations[0])
    weighted = departure / (obs_sigma[0] * obs_sigma[0])

    spread = wy[None] * weighted[:, None, :]
    adjoint = jnp.einsum("zro,co->zrc", spread, wx, precision=hi)
    adjoint = lax.optimization_barrier(adjoint)

    spread_a = pad2(adjoint, 2)
    inner = trim(weights, 1)
    once_n = diffuse(spread_a[:, 0:4], [w[0:2] for w in inner])
    twice_n = diffuse(jnp.pad(once_n, ((0, 0), (2, 0), (2, 2))), [w[0:2] for w in weights])
    once_s = diffuse(spread_a[:, rows : rows + 5], [w[rows : rows + 3] for w in inner])
    twice_s = diffuse(
        jnp.pad(once_s, ((0, 0), (0, 2), (2, 2))), [w[rows + 2 : rows + 5] for w in weights]
    )
    from_south = neighbour_shift(twice_n, 1, 0)
    from_north = neighbour_shift(twice_s, -1, 0)

    once = diffuse(spread_a, inner)
    middle = diffuse(pad2(once, 2)[:, 2 : rows + 4], [w[2 : rows + 2] for w in weights])
    middle = middle.at[:, rows - GN :, :].add(from_south)
    middle = middle.at[:, :GS, :].add(from_north)
    gradient = middle[:, :, GW : GW + cols]
    from_east = neighbour_shift(middle[:, :, :GW], 0, 1)
    from_west = neighbour_shift(middle[:, :, GW + cols :], 0, -1)
    gradient = gradient.at[:, :, cols - GW :].add(from_east)
    gradient = gradient.at[:, :, :GE].add(from_west)
    return gradient, departure[None]


def solution(mesh):
    in_specs = (
        P(None, "lat", "lon"),
        P("lat", "lon"),
        P("lat", "lon"),
        P("lat", None, "lon"),
        P("lat", None, "lon"),
        P("lat", "lon"),
        P("lat", "lon"),
        P("lat", None, "lon"),
        P("lat", "lon"),
    )
    out_specs = (P(None, "lat", "lon"), P("lat", None, "lon"))
    return jax.shard_map(
        on_device, mesh=mesh, in_specs=in_specs, out_specs=out_specs, check_vma=False
    )
```

```python
import jax
import jax.numpy as jnp
from jax import lax
from jax.experimental.layout import Layout, with_layout_constraint
from jax.sharding import PartitionSpec as P

HN, HS, HW, HE = 3, 4, 3, 4
GN, GS, GW, GE = 2, 3, 2, 3


def neighbour_shift(block, dy, dx):
    n_lon = lax.axis_size("lon")
    n_lat = lax.axis_size("lat")
    if dy == 0:
        pairs = [((i + dx) % n_lon, i) for i in range(n_lon)]
        return lax.ppermute(block, "lon", pairs)
    if dx == 0:
        pairs = [(j + dy, j) for j in range(n_lat) if 0 <= j + dy < n_lat]
        return lax.ppermute(block, "lat", pairs)
    pairs = []
    for i in range(n_lon):
        for j in range(n_lat):
            if 0 <= j + dy < n_lat:
                source = ((i + dx) % n_lon) * n_lat + (j + dy)
                pairs.append((source, i * n_lat + j))
    return lax.ppermute(block, ("lon", "lat"), pairs)


def gather_halo(parts, hn, hs, hw, he):
    rows, cols = parts[0].shape[-2:]
    sizes = [p.shape[0] for p in parts]

    def joined(window):
        return jnp.concatenate([p[window] for p in parts], axis=0)

    west = neighbour_shift(joined((Ellipsis, slice(None), slice(cols - hw, None))), 0, -1)
    east = neighbour_shift(joined((Ellipsis, slice(None), slice(0, he))), 0, 1)
    edge_n = jnp.concatenate(
        [west[..., rows - hn :, :], joined((Ellipsis, slice(rows - hn, None), slice(None))),
         east[..., rows - hn :, :]], axis=-1)
    edge_s = jnp.concatenate(
        [west[..., :hs, :], joined((Ellipsis, slice(0, hs), slice(None))), east[..., :hs, :]], axis=-1)
    north = neighbour_shift(edge_n, -1, 0)
    south = neighbour_shift(edge_s, 1, 0)

    out, at = [], 0
    for part, size in zip(parts, sizes):
        span = slice(at, at + size)
        middle = jnp.concatenate([west[span], part, east[span]], axis=-1)
        out.append(jnp.concatenate([north[span], middle, south[span]], axis=-2))
        at += size
    return out


def scatter_halo(g, rows, cols, gn, gs, gw, ge):
    h = g[..., gn : gn + rows, :]
    from_south = neighbour_shift(g[..., :gn, :], 1, 0)
    from_north = neighbour_shift(g[..., gn + rows :, :], -1, 0)
    h = h.at[..., rows - gn :, :].add(from_south)
    h = h.at[..., :gs, :].add(from_north)
    total = h[..., :, gw : gw + cols]
    from_east = neighbour_shift(h[..., :, :gw], 0, 1)
    from_west = neighbour_shift(h[..., :, gw + cols :], 0, -1)
    total = total.at[..., :, cols - gw :].add(from_east)
    total = total.at[..., :, :ge].add(from_west)
    return total


def edge_weights(kappa, mask):
    mid = (slice(1, -1), slice(1, -1))
    kappa_mid = kappa[mid]
    mask_mid = mask[mid]
    out = []
    for oy, ox in ((0, 1), (0, -1), (1, 0), (-1, 0)):
        near = (slice(1 + oy, kappa.shape[0] - 1 + oy), slice(1 + ox, kappa.shape[1] - 1 + ox))
        out.append(0.5 * (kappa_mid + kappa[near]) * mask_mid * mask[near])
    return out


def diffuse(padded, weights):
    center = padded[..., 1:-1, 1:-1]
    result = center
    for (oy, ox), weight in zip(((0, 1), (0, -1), (1, 0), (-1, 0)), weights):
        near = padded[..., 1 + oy : padded.shape[-2] - 1 + oy, 1 + ox : padded.shape[-1] - 1 + ox]
        result = result + weight * (near - center)
    return result


def trim(weights, k):
    return [w[k : w.shape[0] - k, k : w.shape[1] - k] for w in weights]


def pad2(x, k):
    return jnp.pad(x, ((0, 0), (k, k), (k, k)))


def on_device(
    control, diffusivity, land_mask, innovations, obs_sigma, obs_row, obs_col, obs_frac, obs_counts
):
    channels, rows, cols = control.shape
    coeff = jnp.stack([diffusivity, land_mask.astype(jnp.float32)])
    field, coeff = gather_halo([control, coeff], HN, HS, HW, HE)
    field = with_layout_constraint(field, Layout(major_to_minor=(1, 2, 0)))
    weights = edge_weights(coeff[0], coeff[1])

    once = diffuse(field, weights)
    state = diffuse(
        once[:, 1 : rows + 4, 1 : cols + 4], [w[2 : rows + 3, 2 : cols + 3] for w in weights]
    )
    state = lax.optimization_barrier(state)

    frac_y = obs_frac[0, 0]
    frac_x = obs_frac[0, 1]
    row_ids = lax.broadcasted_iota(jnp.int32, (rows + 1, obs_row.shape[1]), 0)
    col_ids = lax.broadcasted_iota(jnp.int32, (cols + 1, obs_col.shape[1]), 0)
    base_r = obs_row[0][None]
    base_c = obs_col[0][None]
    wy = jnp.where(row_ids == base_r, 1.0 - frac_y[None], 0.0) + jnp.where(
        row_ids == base_r + 1, frac_y[None], 0.0
    )
    wx = jnp.where(col_ids == base_c, 1.0 - frac_x[None], 0.0) + jnp.where(
        col_ids == base_c + 1, frac_x[None], 0.0
    )
    hi = lax.Precision.HIGHEST
    along = jnp.einsum("zrc,co->zro", state, wx, precision=hi)
    sample = jnp.sum(along * wy[None], axis=1)

    slots = jnp.arange(obs_row.shape[1], dtype=jnp.int32)
    valid = (slots < obs_counts[0, 0]).astype(jnp.float32)
    departure = valid * (sample - innovations[0])
    weighted = departure / (obs_sigma[0] * obs_sigma[0])

    spread = wy[None] * weighted[:, None, :]
    adjoint = jnp.einsum("zro,co->zrc", spread, wx, precision=hi)
    adjoint = lax.optimization_barrier(adjoint)

    spread_a = pad2(adjoint, 2)
    inner = trim(weights, 1)
    once_n = diffuse(spread_a[:, 0:4], [w[0:2] for w in inner])
    twice_n = diffuse(jnp.pad(once_n, ((0, 0), (2, 0), (2, 2))), [w[0:2] for w in weights])
    once_s = diffuse(spread_a[:, rows : rows + 5], [w[rows : rows + 3] for w in inner])
    twice_s = diffuse(
        jnp.pad(once_s, ((0, 0), (0, 2), (2, 2))), [w[rows + 2 : rows + 5] for w in weights]
    )
    from_south = neighbour_shift(twice_n, 1, 0)
    from_north = neighbour_shift(twice_s, -1, 0)

    once = diffuse(spread_a, inner)
    middle = diffuse(pad2(once, 2)[:, 2 : rows + 4], [w[2 : rows + 2] for w in weights])
    middle = middle.at[:, rows - GN :, :].add(from_south)
    middle = middle.at[:, :GS, :].add(from_north)
    gradient = middle[:, :, GW : GW + cols]
    from_east = neighbour_shift(middle[:, :, :GW], 0, 1)
    from_west = neighbour_shift(middle[:, :, GW + cols :], 0, -1)
    gradient = gradient.at[:, :, cols - GW :].add(from_east)
    gradient = gradient.at[:, :, :GE].add(from_west)
    return gradient, departure[None]


def solution(mesh):
    in_specs = (
        P(None, "lat", "lon"),
        P("lat", "lon"),
        P("lat", "lon"),
        P("lat", None, "lon"),
        P("lat", None, "lon"),
        P("lat", "lon"),
        P("lat", "lon"),
        P("lat", None, "lon"),
        P("lat", "lon"),
    )
    out_specs = (P(None, "lat", "lon"), P("lat", None, "lon"))
    return jax.shard_map(
        on_device, mesh=mesh, in_specs=in_specs, out_specs=out_specs, check_vma=False
    )
```

```python
import jax
import jax.numpy as jnp
from jax import lax
from jax.experimental.layout import Layout, with_layout_constraint
from jax.sharding import PartitionSpec as P

HN, HS, HW, HE = 3, 4, 3, 4
GN, GS, GW, GE = 2, 3, 2, 3


def neighbour_shift(block, dy, dx):
    n_lon = lax.axis_size("lon")
    n_lat = lax.axis_size("lat")
    if dy == 0:
        pairs = [((i + dx) % n_lon, i) for i in range(n_lon)]
        return lax.ppermute(block, "lon", pairs)
    if dx == 0:
        pairs = [(j + dy, j) for j in range(n_lat) if 0 <= j + dy < n_lat]
        return lax.ppermute(block, "lat", pairs)
    pairs = []
    for i in range(n_lon):
        for j in range(n_lat):
            if 0 <= j + dy < n_lat:
                source = ((i + dx) % n_lon) * n_lat + (j + dy)
                pairs.append((source, i * n_lat + j))
    return lax.ppermute(block, ("lon", "lat"), pairs)


def gather_halo(parts, hn, hs, hw, he):
    rows, cols = parts[0].shape[-2:]
    sizes = [p.shape[0] for p in parts]

    def joined(window):
        return jnp.concatenate([p[window] for p in parts], axis=0)

    west = neighbour_shift(joined((Ellipsis, slice(None), slice(cols - hw, None))), 0, -1)
    east = neighbour_shift(joined((Ellipsis, slice(None), slice(0, he))), 0, 1)
    edge_n = jnp.concatenate(
        [west[..., rows - hn :, :], joined((Ellipsis, slice(rows - hn, None), slice(None))),
         east[..., rows - hn :, :]], axis=-1)
    edge_s = jnp.concatenate(
        [west[..., :hs, :], joined((Ellipsis, slice(0, hs), slice(None))), east[..., :hs, :]], axis=-1)
    north = neighbour_shift(edge_n, -1, 0)
    south = neighbour_shift(edge_s, 1, 0)

    out, at = [], 0
    for part, size in zip(parts, sizes):
        span = slice(at, at + size)
        middle = jnp.concatenate([west[span], part, east[span]], axis=-1)
        out.append(jnp.concatenate([north[span], middle, south[span]], axis=-2))
        at += size
    return out


def scatter_halo(g, rows, cols, gn, gs, gw, ge):
    h = g[..., gn : gn + rows, :]
    from_south = neighbour_shift(g[..., :gn, :], 1, 0)
    from_north = neighbour_shift(g[..., gn + rows :, :], -1, 0)
    h = h.at[..., rows - gn :, :].add(from_south)
    h = h.at[..., :gs, :].add(from_north)
    total = h[..., :, gw : gw + cols]
    from_east = neighbour_shift(h[..., :, :gw], 0, 1)
    from_west = neighbour_shift(h[..., :, gw + cols :], 0, -1)
    total = total.at[..., :, cols - gw :].add(from_east)
    total = total.at[..., :, :ge].add(from_west)
    return total


def edge_weights(kappa, mask):
    mid = (slice(1, -1), slice(1, -1))
    kappa_mid = kappa[mid]
    mask_mid = mask[mid]
    out = []
    for oy, ox in ((0, 1), (0, -1), (1, 0), (-1, 0)):
        near = (slice(1 + oy, kappa.shape[0] - 1 + oy), slice(1 + ox, kappa.shape[1] - 1 + ox))
        out.append(0.5 * (kappa_mid + kappa[near]) * mask_mid * mask[near])
    return out


def diffuse(padded, weights):
    center = padded[..., 1:-1, 1:-1]
    result = center
    for (oy, ox), weight in zip(((0, 1), (0, -1), (1, 0), (-1, 0)), weights):
        near = padded[..., 1 + oy : padded.shape[-2] - 1 + oy, 1 + ox : padded.shape[-1] - 1 + ox]
        result = result + weight * (near - center)
    return result


def trim(weights, k):
    return [w[k : w.shape[0] - k, k : w.shape[1] - k] for w in weights]


def pad2(x, k):
    return jnp.pad(x, ((0, 0), (k, k), (k, k)))


def on_device(
    control, diffusivity, land_mask, innovations, obs_sigma, obs_row, obs_col, obs_frac, obs_counts
):
    channels, rows, cols = control.shape
    coeff = jnp.stack([diffusivity, land_mask.astype(jnp.float32)])
    field, coeff = gather_halo([control, coeff], HN, HS, HW, HE)
    field = with_layout_constraint(field, Layout(major_to_minor=(1, 2, 0)))
    weights = edge_weights(coeff[0], coeff[1])

    once = diffuse(field, weights)
    state = diffuse(
        once[:, 1 : rows + 4, 1 : cols + 4], [w[2 : rows + 3, 2 : cols + 3] for w in weights]
    )
    state = lax.optimization_barrier(state)

    frac_y = obs_frac[0, 0]
    frac_x = obs_frac[0, 1]
    row_ids = lax.broadcasted_iota(jnp.int32, (rows + 1, obs_row.shape[1]), 0)
    col_ids = lax.broadcasted_iota(jnp.int32, (cols + 1, obs_col.shape[1]), 0)
    base_r = obs_row[0][None]
    base_c = obs_col[0][None]
    wy = jnp.where(row_ids == base_r, 1.0 - frac_y[None], 0.0) + jnp.where(
        row_ids == base_r + 1, frac_y[None], 0.0
    )
    wx = jnp.where(col_ids == base_c, 1.0 - frac_x[None], 0.0) + jnp.where(
        col_ids == base_c + 1, frac_x[None], 0.0
    )
    hi = lax.Precision.HIGHEST
    along = jnp.einsum("zrc,co->zro", state, wx, precision=hi)
    sample = jnp.sum(along * wy[None], axis=1)

    slots = jnp.arange(obs_row.shape[1], dtype=jnp.int32)
    valid = (slots < obs_counts[0, 0]).astype(jnp.float32)
    departure = valid * (sample - innovations[0])
    weighted = departure / (obs_sigma[0] * obs_sigma[0])

    spread = wy[None] * weighted[:, None, :]
    adjoint = jnp.einsum("zro,co->zrc", spread, wx, precision=hi)
    adjoint = lax.optimization_barrier(adjoint)

    spread_a = pad2(adjoint, 2)
    inner = trim(weights, 1)
    once_n = diffuse(spread_a[:, 0:4], [w[0:2] for w in inner])
    twice_n = diffuse(jnp.pad(once_n, ((0, 0), (2, 0), (2, 2))), [w[0:2] for w in weights])
    once_s = diffuse(spread_a[:, rows : rows + 5], [w[rows : rows + 3] for w in inner])
    twice_s = diffuse(
        jnp.pad(once_s, ((0, 0), (0, 2), (2, 2))), [w[rows + 2 : rows + 5] for w in weights]
    )
    from_south = neighbour_shift(twice_n, 1, 0)
    from_north = neighbour_shift(twice_s, -1, 0)

    once_w = diffuse(spread_a[:, 0 : rows + 4, 0:4], [w[0 : rows + 2, 0:2] for w in inner])
    twice_w = diffuse(
        jnp.pad(once_w, ((0, 0), (0, 0), (2, 0))), [w[2 : rows + 2, 0:2] for w in weights]
    )
    once_e = diffuse(
        spread_a[:, 0 : rows + 4, cols : cols + 5], [w[0 : rows + 2, cols : cols + 3] for w in inner]
    )
    twice_e = diffuse(
        jnp.pad(once_e, ((0, 0), (0, 0), (0, 2))), [w[2 : rows + 2, cols + 2 : cols + 5] for w in weights]
    )
    twice_w = twice_w.at[:, rows - GN :, :].add(from_south[:, :, :GW])
    twice_w = twice_w.at[:, :GS, :].add(from_north[:, :, :GW])
    twice_e = twice_e.at[:, rows - GN :, :].add(from_south[:, :, GW + cols :])
    twice_e = twice_e.at[:, :GS, :].add(from_north[:, :, GW + cols :])
    once = diffuse(spread_a, inner)
    once, twice_w, twice_e = lax.optimization_barrier((once, twice_w, twice_e))
    from_east = neighbour_shift(twice_w, 0, 1)
    from_west = neighbour_shift(twice_e, 0, -1)
    gradient = diffuse(
        pad2(once, 2)[:, 2 : rows + 4, 2 : cols + 4], [w[2 : rows + 2, 2 : cols + 2] for w in weights]
    )
    gradient = gradient.at[:, rows - GN :, :].add(from_south[:, :, GW : GW + cols])
    gradient = gradient.at[:, :GS, :].add(from_north[:, :, GW : GW + cols])
    gradient = gradient.at[:, :, cols - GW :].add(from_east)
    gradient = gradient.at[:, :, :GE].add(from_west)
    return gradient, departure[None]


def solution(mesh):
    in_specs = (
        P(None, "lat", "lon"),
        P("lat", "lon"),
        P("lat", "lon"),
        P("lat", None, "lon"),
        P("lat", None, "lon"),
        P("lat", "lon"),
        P("lat", "lon"),
        P("lat", None, "lon"),
        P("lat", "lon"),
    )
    out_specs = (P(None, "lat", "lon"), P("lat", None, "lon"))
    return jax.shard_map(
        on_device, mesh=mesh, in_specs=in_specs, out_specs=out_specs, check_vma=False
    )
```

```python
import jax
import jax.numpy as jnp
from jax import lax
from jax.experimental.layout import Layout, with_layout_constraint
from jax.sharding import PartitionSpec as P

HN, HS, HW, HE = 3, 4, 3, 4
GN, GS, GW, GE = 2, 3, 2, 3


def neighbour_shift(block, dy, dx):
    n_lon = lax.axis_size("lon")
    n_lat = lax.axis_size("lat")
    if dy == 0:
        pairs = [((i + dx) % n_lon, i) for i in range(n_lon)]
        return lax.ppermute(block, "lon", pairs)
    if dx == 0:
        pairs = [(j + dy, j) for j in range(n_lat) if 0 <= j + dy < n_lat]
        return lax.ppermute(block, "lat", pairs)
    pairs = []
    for i in range(n_lon):
        for j in range(n_lat):
            if 0 <= j + dy < n_lat:
                source = ((i + dx) % n_lon) * n_lat + (j + dy)
                pairs.append((source, i * n_lat + j))
    return lax.ppermute(block, ("lon", "lat"), pairs)


def gather_halo(parts, hn, hs, hw, he):
    rows, cols = parts[0].shape[-2:]
    sizes = [p.shape[0] for p in parts]

    def joined(window):
        return jnp.concatenate([p[window] for p in parts], axis=0)

    west = neighbour_shift(joined((Ellipsis, slice(None), slice(cols - hw, None))), 0, -1)
    east = neighbour_shift(joined((Ellipsis, slice(None), slice(0, he))), 0, 1)
    edge_n = jnp.concatenate(
        [west[..., rows - hn :, :], joined((Ellipsis, slice(rows - hn, None), slice(None))),
         east[..., rows - hn :, :]], axis=-1)
    edge_s = jnp.concatenate(
        [west[..., :hs, :], joined((Ellipsis, slice(0, hs), slice(None))), east[..., :hs, :]], axis=-1)
    north = neighbour_shift(edge_n, -1, 0)
    south = neighbour_shift(edge_s, 1, 0)

    out, at = [], 0
    for part, size in zip(parts, sizes):
        span = slice(at, at + size)
        middle = jnp.concatenate([west[span], part, east[span]], axis=-1)
        out.append(jnp.concatenate([north[span], middle, south[span]], axis=-2))
        at += size
    return out


def scatter_halo(g, rows, cols, gn, gs, gw, ge):
    h = g[..., gn : gn + rows, :]
    from_south = neighbour_shift(g[..., :gn, :], 1, 0)
    from_north = neighbour_shift(g[..., gn + rows :, :], -1, 0)
    h = h.at[..., rows - gn :, :].add(from_south)
    h = h.at[..., :gs, :].add(from_north)
    total = h[..., :, gw : gw + cols]
    from_east = neighbour_shift(h[..., :, :gw], 0, 1)
    from_west = neighbour_shift(h[..., :, gw + cols :], 0, -1)
    total = total.at[..., :, cols - gw :].add(from_east)
    total = total.at[..., :, :ge].add(from_west)
    return total


def edge_weights(kappa, mask):
    mid = (slice(1, -1), slice(1, -1))
    kappa_mid = kappa[mid]
    mask_mid = mask[mid]
    out = []
    for oy, ox in ((0, 1), (0, -1), (1, 0), (-1, 0)):
        near = (slice(1 + oy, kappa.shape[0] - 1 + oy), slice(1 + ox, kappa.shape[1] - 1 + ox))
        out.append(0.5 * (kappa_mid + kappa[near]) * mask_mid * mask[near])
    return out


def diffuse(padded, weights):
    center = padded[..., 1:-1, 1:-1]
    result = center
    for (oy, ox), weight in zip(((0, 1), (0, -1), (1, 0), (-1, 0)), weights):
        near = padded[..., 1 + oy : padded.shape[-2] - 1 + oy, 1 + ox : padded.shape[-1] - 1 + ox]
        result = result + weight * (near - center)
    return result


def trim(weights, k):
    return [w[k : w.shape[0] - k, k : w.shape[1] - k] for w in weights]


def pad2(x, k):
    return jnp.pad(x, ((0, 0), (k, k), (k, k)))


def on_device(
    control, diffusivity, land_mask, innovations, obs_sigma, obs_row, obs_col, obs_frac, obs_counts
):
    channels, rows, cols = control.shape
    coeff = jnp.stack([diffusivity, land_mask.astype(jnp.float32)])
    field, coeff = gather_halo([control, coeff], HN, HS, HW, HE)
    field = with_layout_constraint(field, Layout(major_to_minor=(1, 2, 0)))
    weights = edge_weights(coeff[0], coeff[1])

    once = diffuse(field, weights)
    state = diffuse(
        once[:, 1 : rows + 4, 1 : cols + 4], [w[2 : rows + 3, 2 : cols + 3] for w in weights]
    )
    state = lax.optimization_barrier(state)

    frac_y = obs_frac[0, 0]
    frac_x = obs_frac[0, 1]
    row_ids = lax.broadcasted_iota(jnp.int32, (rows + 1, obs_row.shape[1]), 0)
    col_ids = lax.broadcasted_iota(jnp.int32, (cols + 1, obs_col.shape[1]), 0)
    base_r = obs_row[0][None]
    base_c = obs_col[0][None]
    wy = jnp.where(row_ids == base_r, 1.0 - frac_y[None], 0.0) + jnp.where(
        row_ids == base_r + 1, frac_y[None], 0.0
    )
    wx = jnp.where(col_ids == base_c, 1.0 - frac_x[None], 0.0) + jnp.where(
        col_ids == base_c + 1, frac_x[None], 0.0
    )
    hi = lax.Precision.HIGHEST
    along = jnp.einsum("rcz,co->roz", jnp.transpose(state, (1, 2, 0)), wx, precision=hi)
    sample = jnp.sum(along * wy[:, :, None], axis=0).T

    slots = jnp.arange(obs_row.shape[1], dtype=jnp.int32)
    valid = (slots < obs_counts[0, 0]).astype(jnp.float32)
    departure = valid * (sample - innovations[0])
    weighted = departure / (obs_sigma[0] * obs_sigma[0])

    spread = wy[None] * weighted[:, None, :]
    adjoint = jnp.einsum("zro,co->zrc", spread, wx, precision=hi)
    adjoint = lax.optimization_barrier(adjoint)

    spread_a = pad2(adjoint, 2)
    inner = trim(weights, 1)
    once_n = diffuse(spread_a[:, 0:4], [w[0:2] for w in inner])
    twice_n = diffuse(jnp.pad(once_n, ((0, 0), (2, 0), (2, 2))), [w[0:2] for w in weights])
    once_s = diffuse(spread_a[:, rows : rows + 5], [w[rows : rows + 3] for w in inner])
    twice_s = diffuse(
        jnp.pad(once_s, ((0, 0), (0, 2), (2, 2))), [w[rows + 2 : rows + 5] for w in weights]
    )
    from_south = neighbour_shift(twice_n, 1, 0)
    from_north = neighbour_shift(twice_s, -1, 0)

    once_w = diffuse(spread_a[:, 0 : rows + 4, 0:4], [w[0 : rows + 2, 0:2] for w in inner])
    twice_w = diffuse(
        jnp.pad(once_w, ((0, 0), (0, 0), (2, 0))), [w[2 : rows + 2, 0:2] for w in weights]
    )
    once_e = diffuse(
        spread_a[:, 0 : rows + 4, cols : cols + 5], [w[0 : rows + 2, cols : cols + 3] for w in inner]
    )
    twice_e = diffuse(
        jnp.pad(once_e, ((0, 0), (0, 0), (0, 2))), [w[2 : rows + 2, cols + 2 : cols + 5] for w in weights]
    )
    twice_w = twice_w.at[:, rows - GN :, :].add(from_south[:, :, :GW])
    twice_w = twice_w.at[:, :GS, :].add(from_north[:, :, :GW])
    twice_e = twice_e.at[:, rows - GN :, :].add(from_south[:, :, GW + cols :])
    twice_e = twice_e.at[:, :GS, :].add(from_north[:, :, GW + cols :])
    once = diffuse(spread_a, inner)
    once, twice_w, twice_e = lax.optimization_barrier((once, twice_w, twice_e))
    from_east = neighbour_shift(twice_w, 0, 1)
    from_west = neighbour_shift(twice_e, 0, -1)
    gradient = diffuse(
        pad2(once, 2)[:, 2 : rows + 4, 2 : cols + 4], [w[2 : rows + 2, 2 : cols + 2] for w in weights]
    )
    gradient = gradient.at[:, rows - GN :, :].add(from_south[:, :, GW : GW + cols])
    gradient = gradient.at[:, :GS, :].add(from_north[:, :, GW : GW + cols])
    gradient = gradient.at[:, :, cols - GW :].add(from_east)
    gradient = gradient.at[:, :, :GE].add(from_west)
    return gradient, departure[None]


def solution(mesh):
    in_specs = (
        P(None, "lat", "lon"),
        P("lat", "lon"),
        P("lat", "lon"),
        P("lat", None, "lon"),
        P("lat", None, "lon"),
        P("lat", "lon"),
        P("lat", "lon"),
        P("lat", None, "lon"),
        P("lat", "lon"),
    )
    out_specs = (P(None, "lat", "lon"), P("lat", None, "lon"))
    return jax.shard_map(
        on_device, mesh=mesh, in_specs=in_specs, out_specs=out_specs, check_vma=False
    )
```

```python
import jax
import jax.numpy as jnp
from jax import lax
from jax.experimental.layout import Layout, with_layout_constraint
from jax.sharding import PartitionSpec as P

HN, HS, HW, HE = 3, 4, 3, 4
GN, GS, GW, GE = 2, 3, 2, 3


def neighbour_shift(block, dy, dx):
    n_lon = lax.axis_size("lon")
    n_lat = lax.axis_size("lat")
    if dy == 0:
        pairs = [((i + dx) % n_lon, i) for i in range(n_lon)]
        return lax.ppermute(block, "lon", pairs)
    if dx == 0:
        pairs = [(j + dy, j) for j in range(n_lat) if 0 <= j + dy < n_lat]
        return lax.ppermute(block, "lat", pairs)
    pairs = []
    for i in range(n_lon):
        for j in range(n_lat):
            if 0 <= j + dy < n_lat:
                source = ((i + dx) % n_lon) * n_lat + (j + dy)
                pairs.append((source, i * n_lat + j))
    return lax.ppermute(block, ("lon", "lat"), pairs)


def gather_halo(parts, hn, hs, hw, he, gate):
    rows, cols = parts[0].shape[-2:]
    sizes = [p.shape[0] for p in parts]

    def joined(window):
        return jnp.concatenate([p[window] for p in parts], axis=0)

    west_piece = joined((Ellipsis, slice(None), slice(cols - hw, None)))
    east_piece = joined((Ellipsis, slice(None), slice(0, he)))
    west_piece, east_piece, gate = lax.optimization_barrier((west_piece, east_piece, gate))
    west = neighbour_shift(west_piece, 0, -1)
    east = neighbour_shift(east_piece, 0, 1)
    edge_n = jnp.concatenate(
        [west[..., rows - hn :, :], joined((Ellipsis, slice(rows - hn, None), slice(None))),
         east[..., rows - hn :, :]], axis=-1)
    edge_s = jnp.concatenate(
        [west[..., :hs, :], joined((Ellipsis, slice(0, hs), slice(None))), east[..., :hs, :]], axis=-1)
    north = neighbour_shift(edge_n, -1, 0)
    south = neighbour_shift(edge_s, 1, 0)

    out, at = [], 0
    for part, size in zip(parts, sizes):
        span = slice(at, at + size)
        middle = jnp.concatenate([west[span], part, east[span]], axis=-1)
        out.append(jnp.concatenate([north[span], middle, south[span]], axis=-2))
        at += size
    return out


def scatter_halo(g, rows, cols, gn, gs, gw, ge):
    h = g[..., gn : gn + rows, :]
    from_south = neighbour_shift(g[..., :gn, :], 1, 0)
    from_north = neighbour_shift(g[..., gn + rows :, :], -1, 0)
    h = h.at[..., rows - gn :, :].add(from_south)
    h = h.at[..., :gs, :].add(from_north)
    total = h[..., :, gw : gw + cols]
    from_east = neighbour_shift(h[..., :, :gw], 0, 1)
    from_west = neighbour_shift(h[..., :, gw + cols :], 0, -1)
    total = total.at[..., :, cols - gw :].add(from_east)
    total = total.at[..., :, :ge].add(from_west)
    return total


def edge_weights(kappa, mask):
    mid = (slice(1, -1), slice(1, -1))
    kappa_mid = kappa[mid]
    mask_mid = mask[mid]
    out = []
    for oy, ox in ((0, 1), (0, -1), (1, 0), (-1, 0)):
        near = (slice(1 + oy, kappa.shape[0] - 1 + oy), slice(1 + ox, kappa.shape[1] - 1 + ox))
        out.append(0.5 * (kappa_mid + kappa[near]) * mask_mid * mask[near])
    return out


def diffuse(padded, weights):
    center = padded[..., 1:-1, 1:-1]
    result = center
    for (oy, ox), weight in zip(((0, 1), (0, -1), (1, 0), (-1, 0)), weights):
        near = padded[..., 1 + oy : padded.shape[-2] - 1 + oy, 1 + ox : padded.shape[-1] - 1 + ox]
        result = result + weight * (near - center)
    return result


def trim(weights, k):
    return [w[k : w.shape[0] - k, k : w.shape[1] - k] for w in weights]


def pad2(x, k):
    return jnp.pad(x, ((0, 0), (k, k), (k, k)))


def on_device(
    control, diffusivity, land_mask, innovations, obs_sigma, obs_row, obs_col, obs_frac, obs_counts
):
    channels, rows, cols = control.shape
    coeff = jnp.stack([diffusivity, land_mask.astype(jnp.float32)])
    local_w = edge_weights(coeff[0], coeff[1])
    inside = diffuse(diffuse(control, local_w), trim(local_w, 1))
    field, coeff = gather_halo([control, coeff], HN, HS, HW, HE, inside)
    field = with_layout_constraint(field, Layout(major_to_minor=(1, 2, 0)))
    weights = edge_weights(coeff[0], coeff[1])

    def state_on(r0, r1, c0, c1):
        first = diffuse(
            field[:, r0 - 2 + HN : r1 + 2 + HN, c0 - 2 + HW : c1 + 2 + HW],
            [w[r0 + 1 : r1 + 3, c0 + 1 : c1 + 3] for w in weights],
        )
        return diffuse(first, [w[r0 + 2 : r1 + 2, c0 + 2 : c1 + 2] for w in weights])

    top = state_on(0, 2, 0, cols + 1)
    bottom = state_on(rows - 2, rows + 1, 0, cols + 1)
    left = state_on(2, rows - 2, 0, 2)
    right = state_on(2, rows - 2, cols - 2, cols + 1)
    state = jnp.concatenate(
        [top, jnp.concatenate([left, inside, right], axis=-1), bottom], axis=-2
    )
    state = lax.optimization_barrier(state)

    frac_y = obs_frac[0, 0]
    frac_x = obs_frac[0, 1]
    row_ids = lax.broadcasted_iota(jnp.int32, (rows + 1, obs_row.shape[1]), 0)
    col_ids = lax.broadcasted_iota(jnp.int32, (cols + 1, obs_col.shape[1]), 0)
    base_r = obs_row[0][None]
    base_c = obs_col[0][None]
    wy = jnp.where(row_ids == base_r, 1.0 - frac_y[None], 0.0) + jnp.where(
        row_ids == base_r + 1, frac_y[None], 0.0
    )
    wx = jnp.where(col_ids == base_c, 1.0 - frac_x[None], 0.0) + jnp.where(
        col_ids == base_c + 1, frac_x[None], 0.0
    )
    hi = lax.Precision.HIGHEST
    along = jnp.einsum("zrc,co->zro", state, wx, precision=hi)
    sample = jnp.sum(along * wy[None], axis=1)

    slots = jnp.arange(obs_row.shape[1], dtype=jnp.int32)
    valid = (slots < obs_counts[0, 0]).astype(jnp.float32)
    departure = valid * (sample - innovations[0])
    weighted = departure / (obs_sigma[0] * obs_sigma[0])

    spread = wy[None] * weighted[:, None, :]
    adjoint = jnp.einsum("zro,co->zrc", spread, wx, precision=hi)
    adjoint = lax.optimization_barrier(adjoint)

    spread_a = pad2(adjoint, 2)
    inner = trim(weights, 1)
    once_n = diffuse(spread_a[:, 0:4], [w[0:2] for w in inner])
    twice_n = diffuse(jnp.pad(once_n, ((0, 0), (2, 0), (2, 2))), [w[0:2] for w in weights])
    once_s = diffuse(spread_a[:, rows : rows + 5], [w[rows : rows + 3] for w in inner])
    twice_s = diffuse(
        jnp.pad(once_s, ((0, 0), (0, 2), (2, 2))), [w[rows + 2 : rows + 5] for w in weights]
    )
    from_south = neighbour_shift(twice_n, 1, 0)
    from_north = neighbour_shift(twice_s, -1, 0)

    once_w = diffuse(spread_a[:, 0 : rows + 4, 0:4], [w[0 : rows + 2, 0:2] for w in inner])
    twice_w = diffuse(
        jnp.pad(once_w, ((0, 0), (0, 0), (2, 0))), [w[2 : rows + 2, 0:2] for w in weights]
    )
    once_e = diffuse(
        spread_a[:, 0 : rows + 4, cols : cols + 5], [w[0 : rows + 2, cols : cols + 3] for w in inner]
    )
    twice_e = diffuse(
        jnp.pad(once_e, ((0, 0), (0, 0), (0, 2))), [w[2 : rows + 2, cols + 2 : cols + 5] for w in weights]
    )
    twice_w = twice_w.at[:, rows - GN :, :].add(from_south[:, :, :GW])
    twice_w = twice_w.at[:, :GS, :].add(from_north[:, :, :GW])
    twice_e = twice_e.at[:, rows - GN :, :].add(from_south[:, :, GW + cols :])
    twice_e = twice_e.at[:, :GS, :].add(from_north[:, :, GW + cols :])
    once = diffuse(spread_a, inner)
    once, twice_w, twice_e = lax.optimization_barrier((once, twice_w, twice_e))
    from_east = neighbour_shift(twice_w, 0, 1)
    from_west = neighbour_shift(twice_e, 0, -1)
    gradient = diffuse(
        pad2(once, 2)[:, 2 : rows + 4, 2 : cols + 4], [w[2 : rows + 2, 2 : cols + 2] for w in weights]
    )
    gradient = gradient.at[:, rows - GN :, :].add(from_south[:, :, GW : GW + cols])
    gradient = gradient.at[:, :GS, :].add(from_north[:, :, GW : GW + cols])
    gradient = gradient.at[:, :, cols - GW :].add(from_east)
    gradient = gradient.at[:, :, :GE].add(from_west)
    return gradient, departure[None]


def solution(mesh):
    in_specs = (
        P(None, "lat", "lon"),
        P("lat", "lon"),
        P("lat", "lon"),
        P("lat", None, "lon"),
        P("lat", None, "lon"),
        P("lat", "lon"),
        P("lat", "lon"),
        P("lat", None, "lon"),
        P("lat", "lon"),
    )
    out_specs = (P(None, "lat", "lon"), P("lat", None, "lon"))
    return jax.shard_map(
        on_device, mesh=mesh, in_specs=in_specs, out_specs=out_specs, check_vma=False
    )
```

```python
import jax
import jax.numpy as jnp
from jax import lax
from jax.experimental.layout import Layout, with_layout_constraint
from jax.sharding import PartitionSpec as P

HN, HS, HW, HE = 3, 4, 3, 4
GN, GS, GW, GE = 2, 3, 2, 3


def neighbour_shift(block, dy, dx):
    n_lon = lax.axis_size("lon")
    n_lat = lax.axis_size("lat")
    if dy == 0:
        pairs = [((i + dx) % n_lon, i) for i in range(n_lon)]
        return lax.ppermute(block, "lon", pairs)
    if dx == 0:
        pairs = [(j + dy, j) for j in range(n_lat) if 0 <= j + dy < n_lat]
        return lax.ppermute(block, "lat", pairs)
    pairs = []
    for i in range(n_lon):
        for j in range(n_lat):
            if 0 <= j + dy < n_lat:
                source = ((i + dx) % n_lon) * n_lat + (j + dy)
                pairs.append((source, i * n_lat + j))
    return lax.ppermute(block, ("lon", "lat"), pairs)


def gather_halo(parts, hn, hs, hw, he):
    rows, cols = parts[0].shape[-2:]
    sizes = [p.shape[0] for p in parts]

    def joined(window):
        return jnp.concatenate([p[window] for p in parts], axis=0)

    north = neighbour_shift(joined((Ellipsis, slice(rows - hn, None), slice(None))), -1, 0)
    south = neighbour_shift(joined((Ellipsis, slice(0, hs), slice(None))), 1, 0)
    edge_w = jnp.concatenate(
        [north[..., cols - hw :], joined((Ellipsis, slice(None), slice(cols - hw, None))),
         south[..., cols - hw :]], axis=-2)
    edge_e = jnp.concatenate(
        [north[..., :he], joined((Ellipsis, slice(None), slice(0, he))), south[..., :he]], axis=-2)
    west = neighbour_shift(edge_w, 0, -1)
    east = neighbour_shift(edge_e, 0, 1)

    out, at = [], 0
    for part, size in zip(parts, sizes):
        span = slice(at, at + size)
        middle = jnp.concatenate([north[span], part, south[span]], axis=-2)
        out.append(jnp.concatenate([west[span], middle, east[span]], axis=-1))
        at += size
    return out


def scatter_halo(g, rows, cols, gn, gs, gw, ge):
    h = g[..., gn : gn + rows, :]
    from_south = neighbour_shift(g[..., :gn, :], 1, 0)
    from_north = neighbour_shift(g[..., gn + rows :, :], -1, 0)
    h = h.at[..., rows - gn :, :].add(from_south)
    h = h.at[..., :gs, :].add(from_north)
    total = h[..., :, gw : gw + cols]
    from_east = neighbour_shift(h[..., :, :gw], 0, 1)
    from_west = neighbour_shift(h[..., :, gw + cols :], 0, -1)
    total = total.at[..., :, cols - gw :].add(from_east)
    total = total.at[..., :, :ge].add(from_west)
    return total


def edge_weights(kappa, mask):
    mid = (slice(1, -1), slice(1, -1))
    kappa_mid = kappa[mid]
    mask_mid = mask[mid]
    out = []
    for oy, ox in ((0, 1), (0, -1), (1, 0), (-1, 0)):
        near = (slice(1 + oy, kappa.shape[0] - 1 + oy), slice(1 + ox, kappa.shape[1] - 1 + ox))
        out.append(0.5 * (kappa_mid + kappa[near]) * mask_mid * mask[near])
    return out


def diffuse(padded, weights):
    center = padded[..., 1:-1, 1:-1]
    result = center
    for (oy, ox), weight in zip(((0, 1), (0, -1), (1, 0), (-1, 0)), weights):
        near = padded[..., 1 + oy : padded.shape[-2] - 1 + oy, 1 + ox : padded.shape[-1] - 1 + ox]
        result = result + weight * (near - center)
    return result


def trim(weights, k):
    return [w[k : w.shape[0] - k, k : w.shape[1] - k] for w in weights]


def pad2(x, k):
    return jnp.pad(x, ((0, 0), (k, k), (k, k)))


def on_device(
    control, diffusivity, land_mask, innovations, obs_sigma, obs_row, obs_col, obs_frac, obs_counts
):
    channels, rows, cols = control.shape
    coeff = jnp.stack([diffusivity, land_mask.astype(jnp.float32)])
    field, coeff = gather_halo([control, coeff], HN, HS, HW, HE)
    field = with_layout_constraint(field, Layout(major_to_minor=(1, 2, 0)))
    weights = edge_weights(coeff[0], coeff[1])

    once = diffuse(field, weights)
    state = diffuse(
        once[:, 1 : rows + 4, 1 : cols + 4], [w[2 : rows + 3, 2 : cols + 3] for w in weights]
    )
    state = lax.optimization_barrier(state)

    frac_y = obs_frac[0, 0]
    frac_x = obs_frac[0, 1]
    row_ids = lax.broadcasted_iota(jnp.int32, (rows + 1, obs_row.shape[1]), 0)
    col_ids = lax.broadcasted_iota(jnp.int32, (cols + 1, obs_col.shape[1]), 0)
    base_r = obs_row[0][None]
    base_c = obs_col[0][None]
    wy = jnp.where(row_ids == base_r, 1.0 - frac_y[None], 0.0) + jnp.where(
        row_ids == base_r + 1, frac_y[None], 0.0
    )
    wx = jnp.where(col_ids == base_c, 1.0 - frac_x[None], 0.0) + jnp.where(
        col_ids == base_c + 1, frac_x[None], 0.0
    )
    hi = lax.Precision.HIGHEST
    along = jnp.einsum("zrc,co->zro", state, wx, precision=hi)
    sample = jnp.sum(along * wy[None], axis=1)

    slots = jnp.arange(obs_row.shape[1], dtype=jnp.int32)
    valid = (slots < obs_counts[0, 0]).astype(jnp.float32)
    departure = valid * (sample - innovations[0])
    weighted = departure / (obs_sigma[0] * obs_sigma[0])

    spread = wy[None] * weighted[:, None, :]
    adjoint = jnp.einsum("zro,co->zrc", spread, wx, precision=hi)
    adjoint = lax.optimization_barrier(adjoint)

    spread_a = pad2(adjoint, 2)
    inner = trim(weights, 1)
    once_n = diffuse(spread_a[:, 0:4], [w[0:2] for w in inner])
    twice_n = diffuse(jnp.pad(once_n, ((0, 0), (2, 0), (2, 2))), [w[0:2] for w in weights])
    once_s = diffuse(spread_a[:, rows : rows + 5], [w[rows : rows + 3] for w in inner])
    twice_s = diffuse(
        jnp.pad(once_s, ((0, 0), (0, 2), (2, 2))), [w[rows + 2 : rows + 5] for w in weights]
    )
    from_south = neighbour_shift(twice_n, 1, 0)
    from_north = neighbour_shift(twice_s, -1, 0)

    once_w = diffuse(spread_a[:, 0 : rows + 4, 0:4], [w[0 : rows + 2, 0:2] for w in inner])
    twice_w = diffuse(
        jnp.pad(once_w, ((0, 0), (0, 0), (2, 0))), [w[2 : rows + 2, 0:2] for w in weights]
    )
    once_e = diffuse(
        spread_a[:, 0 : rows + 4, cols : cols + 5], [w[0 : rows + 2, cols : cols + 3] for w in inner]
    )
    twice_e = diffuse(
        jnp.pad(once_e, ((0, 0), (0, 0), (0, 2))), [w[2 : rows + 2, cols + 2 : cols + 5] for w in weights]
    )
    twice_w = twice_w.at[:, rows - GN :, :].add(from_south[:, :, :GW])
    twice_w = twice_w.at[:, :GS, :].add(from_north[:, :, :GW])
    twice_e = twice_e.at[:, rows - GN :, :].add(from_south[:, :, GW + cols :])
    twice_e = twice_e.at[:, :GS, :].add(from_north[:, :, GW + cols :])
    once = diffuse(spread_a, inner)
    once, twice_w, twice_e = lax.optimization_barrier((once, twice_w, twice_e))
    from_east = neighbour_shift(twice_w, 0, 1)
    from_west = neighbour_shift(twice_e, 0, -1)
    gradient = diffuse(
        pad2(once, 2)[:, 2 : rows + 4, 2 : cols + 4], [w[2 : rows + 2, 2 : cols + 2] for w in weights]
    )
    gradient = gradient.at[:, rows - GN :, :].add(from_south[:, :, GW : GW + cols])
    gradient = gradient.at[:, :GS, :].add(from_north[:, :, GW : GW + cols])
    gradient = gradient.at[:, :, cols - GW :].add(from_east)
    gradient = gradient.at[:, :, :GE].add(from_west)
    return gradient, departure[None]


def solution(mesh):
    in_specs = (
        P(None, "lat", "lon"),
        P("lat", "lon"),
        P("lat", "lon"),
        P("lat", None, "lon"),
        P("lat", None, "lon"),
        P("lat", "lon"),
        P("lat", "lon"),
        P("lat", None, "lon"),
        P("lat", "lon"),
    )
    out_specs = (P(None, "lat", "lon"), P("lat", None, "lon"))
    return jax.shard_map(
        on_device, mesh=mesh, in_specs=in_specs, out_specs=out_specs, check_vma=False
    )
```

```python
import jax
import jax.numpy as jnp
from jax import lax
from jax.experimental.layout import Layout, with_layout_constraint
from jax.sharding import PartitionSpec as P

HN, HS, HW, HE = 3, 4, 3, 4
GN, GS, GW, GE = 2, 3, 2, 3


def neighbour_shift(block, dy, dx):
    n_lon = lax.axis_size("lon")
    n_lat = lax.axis_size("lat")
    if dy == 0:
        pairs = [((i + dx) % n_lon, i) for i in range(n_lon)]
        return lax.ppermute(block, "lon", pairs)
    if dx == 0:
        pairs = [(j + dy, j) for j in range(n_lat) if 0 <= j + dy < n_lat]
        return lax.ppermute(block, "lat", pairs)
    pairs = []
    for i in range(n_lon):
        for j in range(n_lat):
            if 0 <= j + dy < n_lat:
                source = ((i + dx) % n_lon) * n_lat + (j + dy)
                pairs.append((source, i * n_lat + j))
    return lax.ppermute(block, ("lon", "lat"), pairs)


def gather_halo(parts, hn, hs, hw, he):
    rows, cols = parts[0].shape[-2:]
    sizes = [p.shape[0] for p in parts]

    def joined(window):
        return jnp.concatenate([p[window] for p in parts], axis=0)

    west = neighbour_shift(joined((Ellipsis, slice(None), slice(cols - hw, None))), 0, -1)
    east = neighbour_shift(joined((Ellipsis, slice(None), slice(0, he))), 0, 1)
    edge_n = jnp.concatenate(
        [west[..., rows - hn :, :], joined((Ellipsis, slice(rows - hn, None), slice(None))),
         east[..., rows - hn :, :]], axis=-1)
    edge_s = jnp.concatenate(
        [west[..., :hs, :], joined((Ellipsis, slice(0, hs), slice(None))), east[..., :hs, :]], axis=-1)
    north = neighbour_shift(edge_n, -1, 0)
    south = neighbour_shift(edge_s, 1, 0)

    out, at = [], 0
    for part, size in zip(parts, sizes):
        span = slice(at, at + size)
        middle = jnp.concatenate([west[span], part, east[span]], axis=-1)
        out.append(jnp.concatenate([north[span], middle, south[span]], axis=-2))
        at += size
    return out


def scatter_halo(g, rows, cols, gn, gs, gw, ge):
    h = g[..., gn : gn + rows, :]
    from_south = neighbour_shift(g[..., :gn, :], 1, 0)
    from_north = neighbour_shift(g[..., gn + rows :, :], -1, 0)
    h = h.at[..., rows - gn :, :].add(from_south)
    h = h.at[..., :gs, :].add(from_north)
    total = h[..., :, gw : gw + cols]
    from_east = neighbour_shift(h[..., :, :gw], 0, 1)
    from_west = neighbour_shift(h[..., :, gw + cols :], 0, -1)
    total = total.at[..., :, cols - gw :].add(from_east)
    total = total.at[..., :, :ge].add(from_west)
    return total


def edge_weights(kappa, mask):
    mid = (slice(1, -1), slice(1, -1))
    kappa_mid = kappa[mid]
    mask_mid = mask[mid]
    out = []
    for oy, ox in ((0, 1), (0, -1), (1, 0), (-1, 0)):
        near = (slice(1 + oy, kappa.shape[0] - 1 + oy), slice(1 + ox, kappa.shape[1] - 1 + ox))
        out.append(0.5 * (kappa_mid + kappa[near]) * mask_mid * mask[near])
    return out


def diffuse(padded, weights):
    center = padded[..., 1:-1, 1:-1]
    result = center
    for (oy, ox), weight in zip(((0, 1), (0, -1), (1, 0), (-1, 0)), weights):
        near = padded[..., 1 + oy : padded.shape[-2] - 1 + oy, 1 + ox : padded.shape[-1] - 1 + ox]
        result = result + weight * (near - center)
    return result


def trim(weights, k):
    return [w[k : w.shape[0] - k, k : w.shape[1] - k] for w in weights]


def pad2(x, k):
    return jnp.pad(x, ((0, 0), (k, k), (k, k)))


def on_device(
    control, diffusivity, land_mask, innovations, obs_sigma, obs_row, obs_col, obs_frac, obs_counts
):
    channels, rows, cols = control.shape
    coeff = jnp.stack([diffusivity, land_mask.astype(jnp.float32)])
    field, coeff = gather_halo([control, coeff], HN, HS, HW, HE)
    field = with_layout_constraint(field, Layout(major_to_minor=(1, 2, 0)))
    weights = edge_weights(coeff[0], coeff[1])

    once = diffuse(field, weights)
    state = diffuse(
        once[:, 1 : rows + 4, 1 : cols + 4], [w[2 : rows + 3, 2 : cols + 3] for w in weights]
    )
    state = lax.optimization_barrier(state)

    frac_y = obs_frac[0, 0]
    frac_x = obs_frac[0, 1]
    row_ids = lax.broadcasted_iota(jnp.int32, (rows + 1, obs_row.shape[1]), 0)
    col_ids = lax.broadcasted_iota(jnp.int32, (cols + 1, obs_col.shape[1]), 0)
    base_r = obs_row[0][None]
    base_c = obs_col[0][None]
    wy = jnp.where(row_ids == base_r, 1.0 - frac_y[None], 0.0) + jnp.where(
        row_ids == base_r + 1, frac_y[None], 0.0
    )
    wx = jnp.where(col_ids == base_c, 1.0 - frac_x[None], 0.0) + jnp.where(
        col_ids == base_c + 1, frac_x[None], 0.0
    )
    hi = lax.Precision.HIGHEST
    stencil = wy[:, None, :] * wx[None, :, :]
    sample = jnp.einsum("zrc,rco->zo", state, stencil, precision=hi)

    slots = jnp.arange(obs_row.shape[1], dtype=jnp.int32)
    valid = (slots < obs_counts[0, 0]).astype(jnp.float32)
    departure = valid * (sample - innovations[0])
    weighted = departure / (obs_sigma[0] * obs_sigma[0])

    adjoint = jnp.einsum("zo,rco->zrc", weighted, stencil, precision=hi)
    adjoint = lax.optimization_barrier(adjoint)

    spread_a = pad2(adjoint, 2)
    inner = trim(weights, 1)
    once_n = diffuse(spread_a[:, 0:4], [w[0:2] for w in inner])
    twice_n = diffuse(jnp.pad(once_n, ((0, 0), (2, 0), (2, 2))), [w[0:2] for w in weights])
    once_s = diffuse(spread_a[:, rows : rows + 5], [w[rows : rows + 3] for w in inner])
    twice_s = diffuse(
        jnp.pad(once_s, ((0, 0), (0, 2), (2, 2))), [w[rows + 2 : rows + 5] for w in weights]
    )
    from_south = neighbour_shift(twice_n, 1, 0)
    from_north = neighbour_shift(twice_s, -1, 0)

    once_w = diffuse(spread_a[:, 0 : rows + 4, 0:4], [w[0 : rows + 2, 0:2] for w in inner])
    twice_w = diffuse(
        jnp.pad(once_w, ((0, 0), (0, 0), (2, 0))), [w[2 : rows + 2, 0:2] for w in weights]
    )
    once_e = diffuse(
        spread_a[:, 0 : rows + 4, cols : cols + 5], [w[0 : rows + 2, cols : cols + 3] for w in inner]
    )
    twice_e = diffuse(
        jnp.pad(once_e, ((0, 0), (0, 0), (0, 2))), [w[2 : rows + 2, cols + 2 : cols + 5] for w in weights]
    )
    twice_w = twice_w.at[:, rows - GN :, :].add(from_south[:, :, :GW])
    twice_w = twice_w.at[:, :GS, :].add(from_north[:, :, :GW])
    twice_e = twice_e.at[:, rows - GN :, :].add(from_south[:, :, GW + cols :])
    twice_e = twice_e.at[:, :GS, :].add(from_north[:, :, GW + cols :])
    once = diffuse(spread_a, inner)
    once, twice_w, twice_e = lax.optimization_barrier((once, twice_w, twice_e))
    from_east = neighbour_shift(twice_w, 0, 1)
    from_west = neighbour_shift(twice_e, 0, -1)
    gradient = diffuse(
        pad2(once, 2)[:, 2 : rows + 4, 2 : cols + 4], [w[2 : rows + 2, 2 : cols + 2] for w in weights]
    )
    gradient = gradient.at[:, rows - GN :, :].add(from_south[:, :, GW : GW + cols])
    gradient = gradient.at[:, :GS, :].add(from_north[:, :, GW : GW + cols])
    gradient = gradient.at[:, :, cols - GW :].add(from_east)
    gradient = gradient.at[:, :, :GE].add(from_west)
    return gradient, departure[None]


def solution(mesh):
    in_specs = (
        P(None, "lat", "lon"),
        P("lat", "lon"),
        P("lat", "lon"),
        P("lat", None, "lon"),
        P("lat", None, "lon"),
        P("lat", "lon"),
        P("lat", "lon"),
        P("lat", None, "lon"),
        P("lat", "lon"),
    )
    out_specs = (P(None, "lat", "lon"), P("lat", None, "lon"))
    return jax.shard_map(
        on_device, mesh=mesh, in_specs=in_specs, out_specs=out_specs, check_vma=False
    )
```

```python
import jax
import jax.numpy as jnp
from jax import lax
from jax.experimental.layout import Layout, with_layout_constraint
from jax.sharding import PartitionSpec as P

HN, HS, HW, HE = 3, 4, 3, 4
GN, GS, GW, GE = 2, 3, 2, 3


def neighbour_shift(block, dy, dx):
    n_lon = lax.axis_size("lon")
    n_lat = lax.axis_size("lat")
    if dy == 0:
        pairs = [((i + dx) % n_lon, i) for i in range(n_lon)]
        return lax.ppermute(block, "lon", pairs)
    if dx == 0:
        pairs = [(j + dy, j) for j in range(n_lat) if 0 <= j + dy < n_lat]
        return lax.ppermute(block, "lat", pairs)
    pairs = []
    for i in range(n_lon):
        for j in range(n_lat):
            if 0 <= j + dy < n_lat:
                source = ((i + dx) % n_lon) * n_lat + (j + dy)
                pairs.append((source, i * n_lat + j))
    return lax.ppermute(block, ("lon", "lat"), pairs)


def gather_halo(parts, hn, hs, hw, he):
    rows, cols = parts[0].shape[-2:]
    sizes = [p.shape[0] for p in parts]

    def joined(window):
        return jnp.concatenate([p[window] for p in parts], axis=0)

    west = neighbour_shift(joined((Ellipsis, slice(None), slice(cols - hw, None))), 0, -1)
    east = neighbour_shift(joined((Ellipsis, slice(None), slice(0, he))), 0, 1)
    edge_n = jnp.concatenate(
        [west[..., rows - hn :, :], joined((Ellipsis, slice(rows - hn, None), slice(None))),
         east[..., rows - hn :, :]], axis=-1)
    edge_s = jnp.concatenate(
        [west[..., :hs, :], joined((Ellipsis, slice(0, hs), slice(None))), east[..., :hs, :]], axis=-1)
    north = neighbour_shift(edge_n, -1, 0)
    south = neighbour_shift(edge_s, 1, 0)

    out, at = [], 0
    for part, size in zip(parts, sizes):
        span = slice(at, at + size)
        middle = jnp.concatenate([west[span], part, east[span]], axis=-1)
        out.append(jnp.concatenate([north[span], middle, south[span]], axis=-2))
        at += size
    return out


def scatter_halo(g, rows, cols, gn, gs, gw, ge):
    h = g[..., gn : gn + rows, :]
    from_south = neighbour_shift(g[..., :gn, :], 1, 0)
    from_north = neighbour_shift(g[..., gn + rows :, :], -1, 0)
    h = h.at[..., rows - gn :, :].add(from_south)
    h = h.at[..., :gs, :].add(from_north)
    total = h[..., :, gw : gw + cols]
    from_east = neighbour_shift(h[..., :, :gw], 0, 1)
    from_west = neighbour_shift(h[..., :, gw + cols :], 0, -1)
    total = total.at[..., :, cols - gw :].add(from_east)
    total = total.at[..., :, :ge].add(from_west)
    return total


def edge_weights(kappa, mask):
    mid = (slice(1, -1), slice(1, -1))
    kappa_mid = kappa[mid]
    mask_mid = mask[mid]
    out = []
    for oy, ox in ((0, 1), (0, -1), (1, 0), (-1, 0)):
        near = (slice(1 + oy, kappa.shape[0] - 1 + oy), slice(1 + ox, kappa.shape[1] - 1 + ox))
        out.append(0.5 * (kappa_mid + kappa[near]) * mask_mid * mask[near])
    return out


def diffuse(padded, weights):
    center = padded[..., 1:-1, 1:-1]
    result = center
    for (oy, ox), weight in zip(((0, 1), (0, -1), (1, 0), (-1, 0)), weights):
        near = padded[..., 1 + oy : padded.shape[-2] - 1 + oy, 1 + ox : padded.shape[-1] - 1 + ox]
        result = result + weight * (near - center)
    return result


def trim(weights, k):
    return [w[k : w.shape[0] - k, k : w.shape[1] - k] for w in weights]


def pad2(x, k):
    return jnp.pad(x, ((0, 0), (k, k), (k, k)))


def on_device(
    control, diffusivity, land_mask, innovations, obs_sigma, obs_row, obs_col, obs_frac, obs_counts
):
    channels, rows, cols = control.shape
    coeff = jnp.stack([diffusivity, land_mask.astype(jnp.float32)])
    field, coeff = gather_halo([control, coeff], HN, HS, HW, HE)
    field = with_layout_constraint(field, Layout(major_to_minor=(1, 2, 0)))
    weights = edge_weights(coeff[0], coeff[1])

    once = diffuse(field, weights)
    state = diffuse(
        once[:, 1 : rows + 4, 1 : cols + 4], [w[2 : rows + 3, 2 : cols + 3] for w in weights]
    )
    state = lax.optimization_barrier(state)

    frac_y = obs_frac[0, 0]
    frac_x = obs_frac[0, 1]
    row_ids = lax.broadcasted_iota(jnp.int32, (rows + 1, obs_row.shape[1]), 0)
    col_ids = lax.broadcasted_iota(jnp.int32, (cols + 1, obs_col.shape[1]), 0)
    base_r = obs_row[0][None]
    base_c = obs_col[0][None]
    wy = jnp.where(row_ids == base_r, 1.0 - frac_y[None], 0.0) + jnp.where(
        row_ids == base_r + 1, frac_y[None], 0.0
    )
    wx = jnp.where(col_ids == base_c, 1.0 - frac_x[None], 0.0) + jnp.where(
        col_ids == base_c + 1, frac_x[None], 0.0
    )
    hi = lax.Precision.HIGHEST
    stencil = wy[:, None, :] * wx[None, :, :]
    sample = jnp.einsum("zrc,rco->zo", state, stencil, precision=hi)

    slots = jnp.arange(obs_row.shape[1], dtype=jnp.int32)
    valid = (slots < obs_counts[0, 0]).astype(jnp.float32)
    departure = valid * (sample - innovations[0])
    weighted = departure / (obs_sigma[0] * obs_sigma[0])

    spread = wy[None] * weighted[:, None, :]
    adjoint = jnp.einsum("zro,co->zrc", spread, wx, precision=hi)
    adjoint = lax.optimization_barrier(adjoint)

    spread_a = pad2(adjoint, 2)
    inner = trim(weights, 1)
    once_n = diffuse(spread_a[:, 0:4], [w[0:2] for w in inner])
    twice_n = diffuse(jnp.pad(once_n, ((0, 0), (2, 0), (2, 2))), [w[0:2] for w in weights])
    once_s = diffuse(spread_a[:, rows : rows + 5], [w[rows : rows + 3] for w in inner])
    twice_s = diffuse(
        jnp.pad(once_s, ((0, 0), (0, 2), (2, 2))), [w[rows + 2 : rows + 5] for w in weights]
    )
    from_south = neighbour_shift(twice_n, 1, 0)
    from_north = neighbour_shift(twice_s, -1, 0)

    once_w = diffuse(spread_a[:, 0 : rows + 4, 0:4], [w[0 : rows + 2, 0:2] for w in inner])
    twice_w = diffuse(
        jnp.pad(once_w, ((0, 0), (0, 0), (2, 0))), [w[2 : rows + 2, 0:2] for w in weights]
    )
    once_e = diffuse(
        spread_a[:, 0 : rows + 4, cols : cols + 5], [w[0 : rows + 2, cols : cols + 3] for w in inner]
    )
    twice_e = diffuse(
        jnp.pad(once_e, ((0, 0), (0, 0), (0, 2))), [w[2 : rows + 2, cols + 2 : cols + 5] for w in weights]
    )
    twice_w = twice_w.at[:, rows - GN :, :].add(from_south[:, :, :GW])
    twice_w = twice_w.at[:, :GS, :].add(from_north[:, :, :GW])
    twice_e = twice_e.at[:, rows - GN :, :].add(from_south[:, :, GW + cols :])
    twice_e = twice_e.at[:, :GS, :].add(from_north[:, :, GW + cols :])
    once = diffuse(spread_a, inner)
    once, twice_w, twice_e = lax.optimization_barrier((once, twice_w, twice_e))
    from_east = neighbour_shift(twice_w, 0, 1)
    from_west = neighbour_shift(twice_e, 0, -1)
    gradient = diffuse(
        pad2(once, 2)[:, 2 : rows + 4, 2 : cols + 4], [w[2 : rows + 2, 2 : cols + 2] for w in weights]
    )
    gradient = gradient.at[:, rows - GN :, :].add(from_south[:, :, GW : GW + cols])
    gradient = gradient.at[:, :GS, :].add(from_north[:, :, GW : GW + cols])
    gradient = gradient.at[:, :, cols - GW :].add(from_east)
    gradient = gradient.at[:, :, :GE].add(from_west)
    return gradient, departure[None]


def solution(mesh):
    in_specs = (
        P(None, "lat", "lon"),
        P("lat", "lon"),
        P("lat", "lon"),
        P("lat", None, "lon"),
        P("lat", None, "lon"),
        P("lat", "lon"),
        P("lat", "lon"),
        P("lat", None, "lon"),
        P("lat", "lon"),
    )
    out_specs = (P(None, "lat", "lon"), P("lat", None, "lon"))
    return jax.shard_map(
        on_device, mesh=mesh, in_specs=in_specs, out_specs=out_specs, check_vma=False
    )
```
